512 devices in a mesh: rc: 64 (over x, y, z_hi), sys: 8 (over z_lo, core).
Axes of the slice: x: 4, y: 4, z: 16 (z_hi: 4, z_lo: 4; z = z_hi * 4 + z_lo), core: 2. Of those that a mesh axis runs over, the one named last changes fastest.
Arguments:
- density: bfloat16 [2, 64, 1600, 512], P(None, 'sys', 'rc'), may hold values from -6 to 6
- system_real: bfloat16 [64, 64], replicated, may hold values from -0.75 to 0.75
- system_imag: bfloat16 [64, 64], replicated, may hold values from -0.75 to 0.75
- left_ham: bfloat16 [40, 40], replicated, may hold values from -1 to 1
- left_coupling: bfloat16 [40, 40], replicated, may hold values from -1 to 1
- right_ham: bfloat16 [40, 40], replicated, may hold values from -1 to 1
- right_coupling: bfloat16 [40, 40], replicated, may hold values from -1 to 1
- left_strength: float32 [64], replicated, may hold values from -1.5 to 1.5
- right_strength: float32 [64], replicated, may hold values from -1.5 to 1.5
- left_damping: float32 [40], replicated, may hold values from 0.1 to 2
- right_damping: float32 [40], replicated, may hold values from 0.1 to 2
- energies: float32 [512], replicated, may hold values from -3 to 3
Outputs:
- derivative: bfloat16 [2, 64, 1600, 512], P(None, 'sys', 'rc')
The draws below stay inside these ranges and needn't reach their ends.
All inputs are finite; a program needn't handle non-finite values.
Results may differ from the reference program's by a relative error of at most 0.0047.
Values may be sent and summed in bfloat16 or wider, within the bound.
No kernel may reach another device: no remote copies, remote signals or barrier semaphores. Data moves between devices by JAX's collectives and lax.ppermute only.
A program may use at most 64 MiB of HBM per device.

```python
import math
import jax
import jax.numpy as jnp
from jax import lax

S = 64
LEV = 40
PAIRS = 1600
COLS = 512


def shard_levels(key, extent, split, low, top_value):
    gain = 1.0
    for dim, parts in split:
        heights = jax.random.uniform(jax.random.fold_in(jax.random.fold_in(key, 6), dim), (parts,), jnp.float32, low / len(split), top_value / len(split))
        gain = gain * jnp.repeat(jnp.exp(heights), extent[dim] // parts).reshape((-1,) + (1,) * (len(extent) - 1 - dim))
    return gain


def normal_values(rng, extent, width, reach, shards=(), held_as=jnp.bfloat16):
    values = jax.random.normal(rng, extent, jnp.float32) * width
    if len(shards) > 0:
        values = shard_levels(rng, extent, shards, -0.22, 0.18) * values
    return jnp.clip(values, min=-reach, max=reach).astype(held_as)


def setup_inputs(seed: int = 0) -> dict:
    key_of = jax.random.split(jax.random.key(seed), 13)
    return {
        "density": normal_values(key_of[0], (2, S, PAIRS, COLS), 1.0, 6.0, ((1, 8), (2, 64))),
        "system_real": normal_values(key_of[1], (S, S), S ** -0.5, 0.75),
        "system_imag": normal_values(key_of[2], (S, S), S ** -0.5, 0.75),
        "left_ham": normal_values(key_of[3], (LEV, LEV), LEV ** -0.5, 1.0),
        "left_coupling": normal_values(key_of[4], (LEV, LEV), LEV ** -0.5, 1.0),
        "right_ham": normal_values(key_of[5], (LEV, LEV), LEV ** -0.5, 1.0),
        "right_coupling": normal_values(key_of[6], (LEV, LEV), LEV ** -0.5, 1.0),
        "left_strength": jnp.clip(jax.random.uniform(key_of[7], (S,), jnp.float32, -1.5, 1.5), -1.5, 1.5),
        "right_strength": jnp.clip(jax.random.uniform(key_of[8], (S,), jnp.float32, -1.5, 1.5), -1.5, 1.5),
        "left_damping": jnp.clip(jnp.exp(jax.random.uniform(key_of[9], (LEV,), jnp.float32, math.log(0.1), math.log(2.0))), 0.1, 2.0),
        "right_damping": jnp.clip(jnp.exp(jax.random.uniform(key_of[10], (LEV,), jnp.float32, math.log(0.1), math.log(2.0))), 0.1, 2.0),
        "energies": jnp.clip(jax.random.uniform(key_of[11], (COLS,), jnp.float32, -3.0, 3.0), -3.0, 3.0),
    }


def symmetric(matrix, factor):
    widened = matrix.astype(jnp.float32)
    return ((widened + factor * widened.T) * 0.5).astype(jnp.bfloat16)


def ladder_terms(block_rows, left_ops, right_ops, left_gain, right_gain):
    item_count, state_count, pair_count, column_count = block_rows.shape
    levels = left_ops.shape[1]
    widened = block_rows.reshape(item_count, state_count, levels, levels * column_count).astype(jnp.float32)
    left_all = jnp.einsum("xa,ksam->ksxm", left_ops.astype(jnp.float32), widened, precision=lax.Precision.HIGHEST)
    left_term = left_all[:, :, :levels] + left_gain[None, :, None, None] * left_all[:, :, levels:]
    deepened = block_rows.reshape(item_count, state_count, levels, levels, column_count).astype(jnp.float32)
    right_all = jnp.einsum("yb,ksabc->ksayc", right_ops.astype(jnp.float32), deepened, precision=lax.Precision.HIGHEST)
    right_term = right_all[:, :, :, :levels] + right_gain[None, :, None, None, None] * right_all[:, :, :, levels:]
    summed = left_term.reshape(item_count, state_count, pair_count, column_count) + right_term.reshape(item_count, state_count, pair_count, column_count)
    return summed.astype(jnp.bfloat16)


def reference(density, system_real, system_imag, left_ham, left_coupling, right_ham, right_coupling, left_strength, right_strength, left_damping, right_damping, energies):
    herm_real = symmetric(system_real, 1.0)
    herm_imag = symmetric(system_imag, -1.0)
    left_ops = jnp.concatenate([symmetric(left_ham, 1.0), symmetric(left_coupling, 1.0)], axis=0)
    right_ops = jnp.concatenate([symmetric(right_ham, 1.0), symmetric(right_coupling, 1.0)], axis=0)
    damping = (0.5 * (left_damping[:, None] + right_damping[None, :])).reshape(PAIRS)
    block_width = math.gcd(COLS, 128)
    block_count = COLS // block_width
    slabs = jnp.moveaxis(density.reshape(2, S, PAIRS, block_count, block_width), 3, 0)
    column_energy = energies.reshape(block_count, block_width)

    def one_block(inputs):
        block_rows, energy_row = inputs
        flattened = block_rows.reshape(2, S, PAIRS * block_width)
        real_part = jnp.dot(herm_real, flattened[0], preferred_element_type=jnp.float32) - jnp.dot(herm_imag, flattened[1], preferred_element_type=jnp.float32)
        imag_part = jnp.dot(herm_real, flattened[1], preferred_element_type=jnp.float32) + jnp.dot(herm_imag, flattened[0], preferred_element_type=jnp.float32)
        system_term = jnp.stack([real_part, imag_part]).astype(jnp.bfloat16).reshape(block_rows.shape).astype(jnp.float32)
        ladder = ladder_terms(block_rows, left_ops, right_ops, left_strength, right_strength).astype(jnp.float32)
        real_in = block_rows[0].astype(jnp.float32)
        imag_in = block_rows[1].astype(jnp.float32)
        energy_grid = energy_row[None, None, :]
        damp_grid = damping[None, :, None]
        new_real = ((system_term[1] + ladder[1]) - energy_grid * imag_in) - damp_grid * real_in
        new_imag = ((-system_term[0] - ladder[0]) + energy_grid * real_in) - damp_grid * imag_in
        return jnp.stack([new_real, new_imag]).astype(jnp.bfloat16)

    result = lax.map(one_block, (slabs, column_energy))
    return jnp.moveaxis(result, 0, 3).reshape(2, S, PAIRS, COLS)
```

```python
import math

import jax
import jax.numpy as jnp
from jax import lax
from jax.sharding import PartitionSpec as P


def symmetric(matrix, factor):
    widened = matrix.astype(jnp.float32)
    return ((widened + factor * widened.T) * 0.5).astype(jnp.bfloat16)


def ladder_local(regrouped, left_ops, right_ops, left_gain, right_gain, levels):
    item_count, group_count, all_pairs, column_count = regrouped.shape
    widened = regrouped.reshape(item_count, group_count, levels, levels * column_count)
    left_all = jnp.einsum("xa,ksam->ksxm", left_ops, widened, preferred_element_type=jnp.float32)
    left_term = left_all[:, :, :levels] + left_gain[None, :, None, None] * left_all[:, :, levels:]
    deepened = regrouped.reshape(item_count, group_count, levels, levels, column_count)
    right_all = jnp.einsum(
        "yb,ksabc->ksayc", right_ops, deepened, preferred_element_type=jnp.float32
    )
    right_term = (
        right_all[:, :, :, :levels]
        + right_gain[None, :, None, None, None] * right_all[:, :, :, levels:]
    )
    summed = left_term.reshape(
        item_count, group_count, all_pairs, column_count
    ) + right_term.reshape(item_count, group_count, all_pairs, column_count)
    return summed.astype(jnp.bfloat16)


def shards(
    density,
    system_real,
    system_imag,
    left_ham,
    left_coupling,
    right_ham,
    right_coupling,
    left_strength,
    right_strength,
    left_damping,
    right_damping,
    energies,
):
    herm_real = symmetric(system_real, 1.0)
    herm_imag = symmetric(system_imag, -1.0)
    levels = left_ham.shape[0]
    left_ops = jnp.concatenate([symmetric(left_ham, 1.0), symmetric(left_coupling, 1.0)], axis=0)
    right_ops = jnp.concatenate([symmetric(right_ham, 1.0), symmetric(right_coupling, 1.0)], axis=0)
    state_count = density.shape[1]
    pair_count = density.shape[2]
    column_total = density.shape[3]
    first_state = lax.axis_index("sys") * state_count
    left_gain = lax.dynamic_slice_in_dim(left_strength, first_state, state_count)
    right_gain = lax.dynamic_slice_in_dim(right_strength, first_state, state_count)
    gathered = lax.all_gather(density, "sys", axis=1, tiled=True)
    own_real = lax.dynamic_slice_in_dim(herm_real, first_state, state_count, axis=0)
    own_imag = lax.dynamic_slice_in_dim(herm_imag, first_state, state_count, axis=0)
    mixer = jnp.concatenate(
        [
            jnp.concatenate([own_real, -own_imag], axis=1),
            jnp.concatenate([own_imag, own_real], axis=1),
        ],
        axis=0,
    )
    stacked = gathered.reshape(2 * gathered.shape[1], -1)
    product = jnp.dot(mixer, stacked, preferred_element_type=jnp.float32)
    system_rows = product.astype(jnp.bfloat16).reshape(density.shape)
    rc_count = lax.axis_size("rc")
    col_groups = rc_count // math.gcd(state_count, rc_count)
    per_device = state_count * col_groups // rc_count
    group_width = column_total // col_groups
    combined = jnp.moveaxis(
        density.reshape(2, state_count, pair_count, col_groups, group_width), 3, 2
    )
    combined = combined.reshape(2, state_count * col_groups, pair_count, group_width)
    combo_index = lax.axis_index("rc") * per_device + jnp.arange(per_device, dtype=jnp.int32)
    state_pick = (
        (combo_index // col_groups)[:, None] == jnp.arange(state_count, dtype=jnp.int32)[None, :]
    ).astype(jnp.float32)
    combo_left = jnp.sum(state_pick * left_gain[None, :], axis=1)
    combo_right = jnp.sum(state_pick * right_gain[None, :], axis=1)
    summed = ladder_local(
        lax.all_to_all(combined, "rc", split_axis=1, concat_axis=2, tiled=True),
        left_ops,
        right_ops,
        combo_left,
        combo_right,
        levels,
    )
    returned = lax.all_to_all(summed, "rc", split_axis=2, concat_axis=1, tiled=True)
    returned = returned.reshape(2, state_count, col_groups, pair_count, group_width)
    ladder_rows = jnp.moveaxis(returned, 2, 3).reshape(2, state_count, pair_count, column_total)
    pair_index = lax.axis_index("rc") * pair_count + jnp.arange(pair_count, dtype=jnp.int32)
    level_index = jnp.arange(levels, dtype=jnp.int32)
    left_pick = (pair_index[:, None] // levels == level_index[None, :]).astype(jnp.float32)
    right_pick = (pair_index[:, None] % levels == level_index[None, :]).astype(jnp.float32)
    damping = 0.5 * (
        jnp.sum(left_pick * left_damping[None, :], axis=1)
        + jnp.sum(right_pick * right_damping[None, :], axis=1)
    )
    system_term = system_rows.astype(jnp.float32)
    ladder = ladder_rows.astype(jnp.float32)
    real_in = density[0].astype(jnp.float32)
    imag_in = density[1].astype(jnp.float32)
    energy_grid = energies[None, None, :]
    damp_grid = damping[None, :, None]
    new_real = system_term[1] + ladder[1] - energy_grid * imag_in - damp_grid * real_in
    new_imag = -system_term[0] - ladder[0] + energy_grid * real_in - damp_grid * imag_in
    return jnp.stack([new_real, new_imag]).astype(jnp.bfloat16)


def solution(mesh):
    placed = (P(None, "sys", "rc", None), P(), P(), P(), P(), P(), P(), P(), P(), P(), P(), P())
    return jax.shard_map(
        shards, mesh=mesh, in_specs=placed, out_specs=P(None, "sys", "rc", None), check_vma=False
    )
```

```python
import math

import jax
import jax.numpy as jnp
from jax import lax
from jax.sharding import PartitionSpec as P


def symmetric(matrix, factor):
    widened = matrix.astype(jnp.float32)
    return ((widened + factor * widened.T) * 0.5).astype(jnp.bfloat16)


def ladder_local(regrouped, left_ops, right_ops, left_gain, right_gain, levels):
    item_count, group_count, all_pairs, column_count = regrouped.shape
    widened = regrouped.reshape(item_count, group_count, levels, levels * column_count)
    left_all = jnp.einsum("xa,ksam->ksxm", left_ops, widened, preferred_element_type=jnp.float32)
    left_term = left_all[:, :, :levels] + left_gain[None, :, None, None] * left_all[:, :, levels:]
    deepened = regrouped.reshape(item_count, group_count, levels, levels, column_count)
    right_all = jnp.einsum(
        "yb,ksabc->ksayc", right_ops, deepened, preferred_element_type=jnp.float32
    )
    right_term = (
        right_all[:, :, :, :levels]
        + right_gain[None, :, None, None, None] * right_all[:, :, :, levels:]
    )
    summed = left_term.reshape(
        item_count, group_count, all_pairs, column_count
    ) + right_term.reshape(item_count, group_count, all_pairs, column_count)
    return summed.astype(jnp.bfloat16)


def shards(
    density,
    system_real,
    system_imag,
    left_ham,
    left_coupling,
    right_ham,
    right_coupling,
    left_strength,
    right_strength,
    left_damping,
    right_damping,
    energies,
):
    herm_real = symmetric(system_real, 1.0)
    herm_imag = symmetric(system_imag, -1.0)
    levels = left_ham.shape[0]
    left_ops = jnp.concatenate([symmetric(left_ham, 1.0), symmetric(left_coupling, 1.0)], axis=0)
    right_ops = jnp.concatenate([symmetric(right_ham, 1.0), symmetric(right_coupling, 1.0)], axis=0)
    state_count = density.shape[1]
    pair_count = density.shape[2]
    column_total = density.shape[3]
    first_state = lax.axis_index("sys") * state_count
    left_gain = lax.dynamic_slice_in_dim(left_strength, first_state, state_count)
    right_gain = lax.dynamic_slice_in_dim(right_strength, first_state, state_count)
    gathered = lax.all_gather(density, "sys", axis=1, tiled=True)
    own_real = lax.dynamic_slice_in_dim(herm_real, first_state, state_count, axis=0)
    own_imag = lax.dynamic_slice_in_dim(herm_imag, first_state, state_count, axis=0)
    mixer = jnp.concatenate(
        [
            jnp.concatenate([own_real, -own_imag], axis=1),
            jnp.concatenate([own_imag, own_real], axis=1),
        ],
        axis=0,
    )
    stacked = gathered.reshape(2 * gathered.shape[1], -1)
    product = jnp.dot(mixer, stacked, preferred_element_type=jnp.float32)
    product = lax.reduce_precision(product, exponent_bits=8, mantissa_bits=7)
    system_rows = product.astype(jnp.bfloat16).reshape(density.shape)
    rc_count = lax.axis_size("rc")
    col_groups = rc_count // state_count
    group_width = column_total // col_groups
    outgoing = density.reshape(2, state_count, pair_count, col_groups, group_width)
    outgoing = jnp.transpose(outgoing, (1, 3, 2, 0, 4)).reshape(
        rc_count, pair_count, 2, group_width
    )
    incoming = lax.all_to_all(outgoing, "rc", split_axis=0, concat_axis=0, tiled=True)
    rows = incoming.reshape(rc_count * pair_count, 2 * group_width).astype(jnp.float32)
    my_state = first_state + lax.axis_index("rc") // col_groups
    left_g = lax.dynamic_slice_in_dim(left_strength, my_state, 1)
    right_g = lax.dynamic_slice_in_dim(right_strength, my_state, 1)
    left_ops32 = left_ops.astype(jnp.float32)
    right_ops32 = right_ops.astype(jnp.float32)
    left_mat = left_ops32[:levels] + left_g * left_ops32[levels:]
    right_mat = right_ops32[:levels] + right_g * right_ops32[levels:]
    left_out = jnp.dot(
        left_mat, rows.reshape(levels, -1), precision=lax.Precision.HIGHEST
    ).reshape(rows.shape)
    block = 8
    block_mat = jnp.kron(jnp.eye(block, dtype=jnp.float32), right_mat)
    chunks = rows.reshape(levels // block, block * levels, -1)
    block_mats = jnp.broadcast_to(block_mat, (levels // block,) + block_mat.shape)
    right_out = jnp.einsum(
        "kpq,kqn->kpn", block_mats, chunks, precision=lax.Precision.HIGHEST
    ).reshape(rows.shape)
    summed = (left_out + right_out).astype(jnp.bfloat16).reshape(outgoing.shape)
    returned = lax.all_to_all(summed, "rc", split_axis=0, concat_axis=0, tiled=True)
    returned = returned.reshape(state_count, col_groups, pair_count, 2, group_width)
    ladder_rows = jnp.transpose(returned, (3, 0, 2, 1, 4)).reshape(density.shape)
    pair_index = lax.axis_index("rc") * pair_count + jnp.arange(pair_count, dtype=jnp.int32)
    level_index = jnp.arange(levels, dtype=jnp.int32)
    left_pick = (pair_index[:, None] // levels == level_index[None, :]).astype(jnp.float32)
    right_pick = (pair_index[:, None] % levels == level_index[None, :]).astype(jnp.float32)
    damping = 0.5 * (
        jnp.sum(left_pick * left_damping[None, :], axis=1)
        + jnp.sum(right_pick * right_damping[None, :], axis=1)
    )
    system_term = system_rows.astype(jnp.float32)
    ladder = ladder_rows.astype(jnp.float32)
    real_in = density[0].astype(jnp.float32)
    imag_in = density[1].astype(jnp.float32)
    energy_grid = energies[None, None, :]
    damp_grid = damping[None, :, None]
    new_real = system_term[1] + ladder[1] - energy_grid * imag_in - damp_grid * real_in
    new_imag = -system_term[0] - ladder[0] + energy_grid * real_in - damp_grid * imag_in
    return jnp.stack([new_real, new_imag]).astype(jnp.bfloat16)


def solution(mesh):
    placed = (P(None, "sys", "rc", None), P(), P(), P(), P(), P(), P(), P(), P(), P(), P(), P())
    return jax.shard_map(
        shards, mesh=mesh, in_specs=placed, out_specs=P(None, "sys", "rc", None), check_vma=False
    )
```

```python
import math

import jax
import jax.numpy as jnp
from jax import lax
from jax.sharding import PartitionSpec as P


def symmetric(matrix, factor):
    widened = matrix.astype(jnp.float32)
    return ((widened + factor * widened.T) * 0.5).astype(jnp.bfloat16)


def ladder_local(regrouped, left_ops, right_ops, left_gain, right_gain, levels):
    item_count, group_count, all_pairs, column_count = regrouped.shape
    widened = regrouped.reshape(item_count, group_count, levels, levels * column_count)
    left_all = jnp.einsum("xa,ksam->ksxm", left_ops, widened, preferred_element_type=jnp.float32)
    left_term = left_all[:, :, :levels] + left_gain[None, :, None, None] * left_all[:, :, levels:]
    deepened = regrouped.reshape(item_count, group_count, levels, levels, column_count)
    right_all = jnp.einsum(
        "yb,ksabc->ksayc", right_ops, deepened, preferred_element_type=jnp.float32
    )
    right_term = (
        right_all[:, :, :, :levels]
        + right_gain[None, :, None, None, None] * right_all[:, :, :, levels:]
    )
    summed = left_term.reshape(
        item_count, group_count, all_pairs, column_count
    ) + right_term.reshape(item_count, group_count, all_pairs, column_count)
    return summed.astype(jnp.bfloat16)


def shards(
    density,
    system_real,
    system_imag,
    left_ham,
    left_coupling,
    right_ham,
    right_coupling,
    left_strength,
    right_strength,
    left_damping,
    right_damping,
    energies,
):
    herm_real = symmetric(system_real, 1.0)
    herm_imag = symmetric(system_imag, -1.0)
    levels = left_ham.shape[0]
    left_ops = jnp.concatenate([symmetric(left_ham, 1.0), symmetric(left_coupling, 1.0)], axis=0)
    right_ops = jnp.concatenate([symmetric(right_ham, 1.0), symmetric(right_coupling, 1.0)], axis=0)
    state_count = density.shape[1]
    pair_count = density.shape[2]
    column_total = density.shape[3]
    first_state = lax.axis_index("sys") * state_count
    left_gain = lax.dynamic_slice_in_dim(left_strength, first_state, state_count)
    right_gain = lax.dynamic_slice_in_dim(right_strength, first_state, state_count)
    gathered = lax.all_gather(density, "sys", axis=1, tiled=True)
    own_real = lax.dynamic_slice_in_dim(herm_real, first_state, state_count, axis=0)
    own_imag = lax.dynamic_slice_in_dim(herm_imag, first_state, state_count, axis=0)
    mixer = jnp.concatenate(
        [
            jnp.concatenate([own_real, -own_imag], axis=1),
            jnp.concatenate([own_imag, own_real], axis=1),
        ],
        axis=0,
    )
    stacked = gathered.reshape(2 * gathered.shape[1], -1)
    product = jnp.dot(mixer, stacked, preferred_element_type=jnp.float32)
    product = lax.reduce_precision(product, exponent_bits=8, mantissa_bits=7)
    system_rows = product.astype(jnp.bfloat16).reshape(density.shape)
    rc_count = lax.axis_size("rc")
    col_groups = rc_count // state_count
    group_width = column_total // col_groups
    my_state = first_state + lax.axis_index("rc") // col_groups
    left_g = lax.dynamic_slice_in_dim(left_strength, my_state, 1)
    right_g = lax.dynamic_slice_in_dim(right_strength, my_state, 1)
    left_ops32 = left_ops.astype(jnp.float32)
    right_ops32 = right_ops.astype(jnp.float32)
    left_mat = left_ops32[:levels] + left_g * left_ops32[levels:]
    right_mat = right_ops32[:levels] + right_g * right_ops32[levels:]
    block = 8
    block_mat = jnp.kron(jnp.eye(block, dtype=jnp.float32), right_mat)
    block_mats = jnp.broadcast_to(block_mat, (levels // block,) + block_mat.shape)
    ladder_parts = []
    for item in range(2):
        outgoing = density[item].reshape(state_count, pair_count, col_groups, group_width)
        outgoing = jnp.transpose(outgoing, (0, 2, 1, 3)).reshape(
            rc_count, pair_count, group_width
        )
        incoming = lax.all_to_all(outgoing, "rc", split_axis=0, concat_axis=0, tiled=True)
        rows = incoming.reshape(rc_count * pair_count, group_width).astype(jnp.float32)
        left_out = jnp.dot(
            left_mat, rows.reshape(levels, -1), precision=lax.Precision.HIGHEST
        ).reshape(rows.shape)
        chunks = rows.reshape(levels // block, block * levels, -1)
        right_out = jnp.einsum(
            "kpq,kqn->kpn", block_mats, chunks, precision=lax.Precision.HIGHEST
        ).reshape(rows.shape)
        summed = (left_out + right_out).astype(jnp.bfloat16).reshape(outgoing.shape)
        returned = lax.all_to_all(summed, "rc", split_axis=0, concat_axis=0, tiled=True)
        returned = returned.reshape(state_count, col_groups, pair_count, group_width)
        ladder_parts.append(
            jnp.transpose(returned, (0, 2, 1, 3)).reshape(density.shape[1:])
        )
    ladder_rows = jnp.stack(ladder_parts)
    pair_index = lax.axis_index("rc") * pair_count + jnp.arange(pair_count, dtype=jnp.int32)
    level_index = jnp.arange(levels, dtype=jnp.int32)
    left_pick = (pair_index[:, None] // levels == level_index[None, :]).astype(jnp.float32)
    right_pick = (pair_index[:, None] % levels == level_index[None, :]).astype(jnp.float32)
    damping = 0.5 * (
        jnp.sum(left_pick * left_damping[None, :], axis=1)
        + jnp.sum(right_pick * right_damping[None, :], axis=1)
    )
    system_term = system_rows.astype(jnp.float32)
    ladder = ladder_rows.astype(jnp.float32)
    real_in = density[0].astype(jnp.float32)
    imag_in = density[1].astype(jnp.float32)
    energy_grid = energies[None, None, :]
    damp_grid = damping[None, :, None]
    new_real = system_term[1] + ladder[1] - energy_grid * imag_in - damp_grid * real_in
    new_imag = -system_term[0] - ladder[0] + energy_grid * real_in - damp_grid * imag_in
    return jnp.stack([new_real, new_imag]).astype(jnp.bfloat16)


def solution(mesh):
    placed = (P(None, "sys", "rc", None), P(), P(), P(), P(), P(), P(), P(), P(), P(), P(), P())
    return jax.shard_map(
        shards, mesh=mesh, in_specs=placed, out_specs=P(None, "sys", "rc", None), check_vma=False
    )
```

```python
import math

import jax
import jax.numpy as jnp
from jax import lax
from jax.sharding import PartitionSpec as P


def symmetric(matrix, factor):
    widened = matrix.astype(jnp.float32)
    return ((widened + factor * widened.T) * 0.5).astype(jnp.bfloat16)


def ladder_local(regrouped, left_ops, right_ops, left_gain, right_gain, levels):
    item_count, group_count, all_pairs, column_count = regrouped.shape
    widened = regrouped.reshape(item_count, group_count, levels, levels * column_count)
    left_all = jnp.einsum("xa,ksam->ksxm", left_ops, widened, preferred_element_type=jnp.float32)
    left_term = left_all[:, :, :levels] + left_gain[None, :, None, None] * left_all[:, :, levels:]
    deepened = regrouped.reshape(item_count, group_count, levels, levels, column_count)
    right_all = jnp.einsum(
        "yb,ksabc->ksayc", right_ops, deepened, preferred_element_type=jnp.float32
    )
    right_term = (
        right_all[:, :, :, :levels]
        + right_gain[None, :, None, None, None] * right_all[:, :, :, levels:]
    )
    summed = left_term.reshape(
        item_count, group_count, all_pairs, column_count
    ) + right_term.reshape(item_count, group_count, all_pairs, column_count)
    return summed.astype(jnp.bfloat16)


def shards(
    density,
    system_real,
    system_imag,
    left_ham,
    left_coupling,
    right_ham,
    right_coupling,
    left_strength,
    right_strength,
    left_damping,
    right_damping,
    energies,
):
    herm_real = symmetric(system_real, 1.0)
    herm_imag = symmetric(system_imag, -1.0)
    levels = left_ham.shape[0]
    left_ops = jnp.concatenate([symmetric(left_ham, 1.0), symmetric(left_coupling, 1.0)], axis=0)
    right_ops = jnp.concatenate([symmetric(right_ham, 1.0), symmetric(right_coupling, 1.0)], axis=0)
    state_count = density.shape[1]
    pair_count = density.shape[2]
    column_total = density.shape[3]
    first_state = lax.axis_index("sys") * state_count
    left_gain = lax.dynamic_slice_in_dim(left_strength, first_state, state_count)
    right_gain = lax.dynamic_slice_in_dim(right_strength, first_state, state_count)
    flat_local = jnp.transpose(density.reshape(2, state_count, -1), (1, 0, 2))
    gathered = lax.all_gather(flat_local.reshape(2 * state_count, -1), "sys", axis=0, tiled=True)
    own_real = lax.dynamic_slice_in_dim(herm_real, first_state, state_count, axis=0)
    own_imag = lax.dynamic_slice_in_dim(herm_imag, first_state, state_count, axis=0)
    real_rows = jnp.stack([own_real, -own_imag], axis=2).reshape(state_count, -1)
    imag_rows = jnp.stack([own_imag, own_real], axis=2).reshape(state_count, -1)
    mixer = jnp.concatenate([real_rows, imag_rows], axis=0)
    product = jnp.dot(mixer, gathered, preferred_element_type=jnp.float32)
    product = lax.reduce_precision(product, exponent_bits=8, mantissa_bits=7)
    system_rows = product.astype(jnp.bfloat16).reshape(density.shape)
    rc_count = lax.axis_size("rc")
    col_groups = rc_count // state_count
    group_width = column_total // col_groups
    outgoing = density.reshape(2, state_count, pair_count, col_groups, group_width)
    outgoing = jnp.transpose(outgoing, (1, 3, 2, 0, 4)).reshape(
        rc_count, pair_count, 2, group_width
    )
    incoming = lax.all_to_all(outgoing, "rc", split_axis=0, concat_axis=0, tiled=True)
    rows = incoming.reshape(rc_count * pair_count, 2 * group_width).astype(jnp.float32)
    my_state = first_state + lax.axis_index("rc") // col_groups
    left_g = lax.dynamic_slice_in_dim(left_strength, my_state, 1)
    right_g = lax.dynamic_slice_in_dim(right_strength, my_state, 1)
    left_ops32 = left_ops.astype(jnp.float32)
    right_ops32 = right_ops.astype(jnp.float32)
    left_mat = left_ops32[:levels] + left_g * left_ops32[levels:]
    right_mat = right_ops32[:levels] + right_g * right_ops32[levels:]
    left_out = jnp.dot(
        left_mat, rows.reshape(levels, -1), precision=lax.Precision.HIGHEST
    ).reshape(rows.shape)
    block = 8
    block_mat = jnp.kron(jnp.eye(block, dtype=jnp.float32), right_mat)
    chunks = rows.reshape(levels // block, block * levels, -1)
    block_mats = jnp.broadcast_to(block_mat, (levels // block,) + block_mat.shape)
    right_out = jnp.einsum(
        "kpq,kqn->kpn", block_mats, chunks, precision=lax.Precision.HIGHEST
    ).reshape(rows.shape)
    summed = (left_out + right_out).astype(jnp.bfloat16).reshape(outgoing.shape)
    returned = lax.all_to_all(summed, "rc", split_axis=0, concat_axis=0, tiled=True)
    returned = returned.reshape(state_count, col_groups, pair_count, 2, group_width)
    ladder_rows = jnp.transpose(returned, (3, 0, 2, 1, 4)).reshape(density.shape)
    pair_index = lax.axis_index("rc") * pair_count + jnp.arange(pair_count, dtype=jnp.int32)
    level_index = jnp.arange(levels, dtype=jnp.int32)
    left_pick = (pair_index[:, None] // levels == level_index[None, :]).astype(jnp.float32)
    right_pick = (pair_index[:, None] % levels == level_index[None, :]).astype(jnp.float32)
    damping = 0.5 * (
        jnp.sum(left_pick * left_damping[None, :], axis=1)
        + jnp.sum(right_pick * right_damping[None, :], axis=1)
    )
    system_term = system_rows.astype(jnp.float32)
    ladder = ladder_rows.astype(jnp.float32)
    real_in = density[0].astype(jnp.float32)
    imag_in = density[1].astype(jnp.float32)
    energy_grid = energies[None, None, :]
    damp_grid = damping[None, :, None]
    new_real = system_term[1] + ladder[1] - energy_grid * imag_in - damp_grid * real_in
    new_imag = -system_term[0] - ladder[0] + energy_grid * real_in - damp_grid * imag_in
    return jnp.stack([new_real, new_imag]).astype(jnp.bfloat16)


def solution(mesh):
    placed = (P(None, "sys", "rc", None), P(), P(), P(), P(), P(), P(), P(), P(), P(), P(), P())
    return jax.shard_map(
        shards, mesh=mesh, in_specs=placed, out_specs=P(None, "sys", "rc", None), check_vma=False
    )
```

```python
import math

import jax
import jax.numpy as jnp
from jax import lax
from jax.sharding import PartitionSpec as P


def symmetric(matrix, factor):
    widened = matrix.astype(jnp.float32)
    return ((widened + factor * widened.T) * 0.5).astype(jnp.bfloat16)


def ladder_local(regrouped, left_ops, right_ops, left_gain, right_gain, levels):
    item_count, group_count, all_pairs, column_count = regrouped.shape
    widened = regrouped.reshape(item_count, group_count, levels, levels * column_count)
    left_all = jnp.einsum("xa,ksam->ksxm", left_ops, widened, preferred_element_type=jnp.float32)
    left_term = left_all[:, :, :levels] + left_gain[None, :, None, None] * left_all[:, :, levels:]
    deepened = regrouped.reshape(item_count, group_count, levels, levels, column_count)
    right_all = jnp.einsum(
        "yb,ksabc->ksayc", right_ops, deepened, preferred_element_type=jnp.float32
    )
    right_term = (
        right_all[:, :, :, :levels]
        + right_gain[None, :, None, None, None] * right_all[:, :, :, levels:]
    )
    summed = left_term.reshape(
        item_count, group_count, all_pairs, column_count
    ) + right_term.reshape(item_count, group_count, all_pairs, column_count)
    return summed.astype(jnp.bfloat16)


def shards(
    density,
    system_real,
    system_imag,
    left_ham,
    left_coupling,
    right_ham,
    right_coupling,
    left_strength,
    right_strength,
    left_damping,
    right_damping,
    energies,
):
    herm_real = symmetric(system_real, 1.0)
    herm_imag = symmetric(system_imag, -1.0)
    levels = left_ham.shape[0]
    left_ops = jnp.concatenate([symmetric(left_ham, 1.0), symmetric(left_coupling, 1.0)], axis=0)
    right_ops = jnp.concatenate([symmetric(right_ham, 1.0), symmetric(right_coupling, 1.0)], axis=0)
    state_count = density.shape[1]
    pair_count = density.shape[2]
    column_total = density.shape[3]
    first_state = lax.axis_index("sys") * state_count
    left_gain = lax.dynamic_slice_in_dim(left_strength, first_state, state_count)
    right_gain = lax.dynamic_slice_in_dim(right_strength, first_state, state_count)
    flat_local = jnp.transpose(density.reshape(2, state_count, -1), (1, 0, 2))
    gathered = lax.all_gather(flat_local.reshape(2 * state_count, -1), "sys", axis=0, tiled=True)
    own_real = lax.dynamic_slice_in_dim(herm_real, first_state, state_count, axis=0)
    own_imag = lax.dynamic_slice_in_dim(herm_imag, first_state, state_count, axis=0)
    real_rows = jnp.stack([own_real, -own_imag], axis=2).reshape(state_count, -1)
    imag_rows = jnp.stack([own_imag, own_real], axis=2).reshape(state_count, -1)
    mixer = jnp.concatenate([real_rows, imag_rows], axis=0)
    product = jnp.dot(mixer, gathered, preferred_element_type=jnp.float32)
    product = lax.reduce_precision(product, exponent_bits=8, mantissa_bits=7)
    system_rows = product.astype(jnp.bfloat16).reshape(density.shape)
    rc_count = lax.axis_size("rc")
    col_groups = rc_count // state_count
    group_width = column_total // col_groups
    outgoing = density.reshape(2, state_count, pair_count, col_groups, group_width)
    outgoing = jnp.transpose(outgoing, (1, 3, 2, 0, 4)).reshape(
        rc_count, pair_count, 2, group_width
    )
    incoming = lax.all_to_all(outgoing, "rc", split_axis=0, concat_axis=0, tiled=True)
    rows = incoming.reshape(rc_count * pair_count, 2 * group_width).astype(jnp.float32)
    my_state = first_state + lax.axis_index("rc") // col_groups
    left_g = lax.dynamic_slice_in_dim(left_strength, my_state, 1)
    right_g = lax.dynamic_slice_in_dim(right_strength, my_state, 1)
    left_ops32 = left_ops.astype(jnp.float32)
    right_ops32 = right_ops.astype(jnp.float32)
    left_mat = left_ops32[:levels] + left_g * left_ops32[levels:]
    right_mat = right_ops32[:levels] + right_g * right_ops32[levels:]
    cube = rows.reshape(levels, levels, -1)
    left_out = jnp.einsum(
        "xa,abn->xbn", left_mat, cube, precision=lax.Precision.HIGHEST
    ).reshape(rows.shape)
    right_mats = jnp.broadcast_to(right_mat, (levels,) + right_mat.shape)
    right_out = jnp.einsum(
        "ayb,abn->ayn", right_mats, cube, precision=lax.Precision.HIGHEST
    ).reshape(rows.shape)
    summed = (left_out + right_out).astype(jnp.bfloat16).reshape(outgoing.shape)
    returned = lax.all_to_all(summed, "rc", split_axis=0, concat_axis=0, tiled=True)
    returned = returned.reshape(state_count, col_groups, pair_count, 2, group_width)
    ladder_rows = jnp.transpose(returned, (3, 0, 2, 1, 4)).reshape(density.shape)
    pair_index = lax.axis_index("rc") * pair_count + jnp.arange(pair_count, dtype=jnp.int32)
    level_index = jnp.arange(levels, dtype=jnp.int32)
    left_pick = (pair_index[:, None] // levels == level_index[None, :]).astype(jnp.float32)
    right_pick = (pair_index[:, None] % levels == level_index[None, :]).astype(jnp.float32)
    damping = 0.5 * (
        jnp.sum(left_pick * left_damping[None, :], axis=1)
        + jnp.sum(right_pick * right_damping[None, :], axis=1)
    )
    system_term = system_rows.astype(jnp.float32)
    ladder = ladder_rows.astype(jnp.float32)
    real_in = density[0].astype(jnp.float32)
    imag_in = density[1].astype(jnp.float32)
    energy_grid = energies[None, None, :]
    damp_grid = damping[None, :, None]
    new_real = system_term[1] + ladder[1] - energy_grid * imag_in - damp_grid * real_in
    new_imag = -system_term[0] - ladder[0] + energy_grid * real_in - damp_grid * imag_in
    return jnp.stack([new_real, new_imag]).astype(jnp.bfloat16)


def solution(mesh):
    placed = (P(None, "sys", "rc", None), P(), P(), P(), P(), P(), P(), P(), P(), P(), P(), P())
    return jax.shard_map(
        shards, mesh=mesh, in_specs=placed, out_specs=P(None, "sys", "rc", None), check_vma=False
    )
```

```python
import math

import jax
import jax.numpy as jnp
from jax import lax
from jax.sharding import PartitionSpec as P


def symmetric(matrix, factor):
    widened = matrix.astype(jnp.float32)
    return ((widened + factor * widened.T) * 0.5).astype(jnp.bfloat16)


def ladder_local(regrouped, left_ops, right_ops, left_gain, right_gain, levels):
    item_count, group_count, all_pairs, column_count = regrouped.shape
    widened = regrouped.reshape(item_count, group_count, levels, levels * column_count)
    left_all = jnp.einsum("xa,ksam->ksxm", left_ops, widened, preferred_element_type=jnp.float32)
    left_term = left_all[:, :, :levels] + left_gain[None, :, None, None] * left_all[:, :, levels:]
    deepened = regrouped.reshape(item_count, group_count, levels, levels, column_count)
    right_all = jnp.einsum(
        "yb,ksabc->ksayc", right_ops, deepened, preferred_element_type=jnp.float32
    )
    right_term = (
        right_all[:, :, :, :levels]
        + right_gain[None, :, None, None, None] * right_all[:, :, :, levels:]
    )
    summed = left_term.reshape(
        item_count, group_count, all_pairs, column_count
    ) + right_term.reshape(item_count, group_count, all_pairs, column_count)
    return summed.astype(jnp.bfloat16)


def shards(
    density,
    system_real,
    system_imag,
    left_ham,
    left_coupling,
    right_ham,
    right_coupling,
    left_strength,
    right_strength,
    left_damping,
    right_damping,
    energies,
):
    herm_real = symmetric(system_real, 1.0)
    herm_imag = symmetric(system_imag, -1.0)
    levels = left_ham.shape[0]
    left_ops = jnp.concatenate([symmetric(left_ham, 1.0), symmetric(left_coupling, 1.0)], axis=0)
    right_ops = jnp.concatenate([symmetric(right_ham, 1.0), symmetric(right_coupling, 1.0)], axis=0)
    state_count = density.shape[1]
    pair_count = density.shape[2]
    column_total = density.shape[3]
    first_state = lax.axis_index("sys") * state_count
    left_gain = lax.dynamic_slice_in_dim(left_strength, first_state, state_count)
    right_gain = lax.dynamic_slice_in_dim(right_strength, first_state, state_count)
    flat_local = jnp.transpose(density.reshape(2, state_count, -1), (1, 0, 2))
    local_rows = flat_local.reshape(2 * state_count, -1)
    sys_count = lax.axis_size("sys")
    blocks = [local_rows]
    for shift in range(1, sys_count):
        pairs = [(i, (i + shift) % sys_count) for i in range(sys_count)]
        blocks.append(lax.ppermute(local_rows, "sys", perm=pairs))
    gathered = jnp.concatenate(blocks, axis=0)
    own_real = lax.dynamic_slice_in_dim(herm_real, first_state, state_count, axis=0)
    own_imag = lax.dynamic_slice_in_dim(herm_imag, first_state, state_count, axis=0)
    real_rows = jnp.stack([own_real, -own_imag], axis=2).reshape(state_count, -1)
    imag_rows = jnp.stack([own_imag, own_real], axis=2).reshape(state_count, -1)
    mixer = jnp.concatenate([real_rows, imag_rows], axis=0)
    mixer = mixer.reshape(2 * state_count, sys_count, 2 * state_count)
    me = lax.axis_index("sys")
    sources = (me - jnp.arange(sys_count, dtype=jnp.int32)) % sys_count
    mixer = jnp.take(mixer, sources, axis=1).reshape(2 * state_count, -1)
    product = jnp.dot(mixer, gathered, preferred_element_type=jnp.float32)
    product = lax.reduce_precision(product, exponent_bits=8, mantissa_bits=7)
    system_rows = product.astype(jnp.bfloat16).reshape(density.shape)
    rc_count = lax.axis_size("rc")
    col_groups = rc_count // state_count
    group_width = column_total // col_groups
    outgoing = density.reshape(2, state_count, pair_count, col_groups, group_width)
    outgoing = jnp.transpose(outgoing, (1, 3, 2, 0, 4)).reshape(
        rc_count, pair_count, 2, group_width
    )
    incoming = lax.all_to_all(outgoing, "rc", split_axis=0, concat_axis=0, tiled=True)
    rows = incoming.reshape(rc_count * pair_count, 2 * group_width).astype(jnp.float32)
    my_state = first_state + lax.axis_index("rc") // col_groups
    left_g = lax.dynamic_slice_in_dim(left_strength, my_state, 1)
    right_g = lax.dynamic_slice_in_dim(right_strength, my_state, 1)
    left_ops32 = left_ops.astype(jnp.float32)
    right_ops32 = right_ops.astype(jnp.float32)
    left_mat = left_ops32[:levels] + left_g * left_ops32[levels:]
    right_mat = right_ops32[:levels] + right_g * right_ops32[levels:]
    cube = rows.reshape(levels, levels, -1)
    left_out = jnp.einsum(
        "xa,abn->xbn", left_mat, cube, precision=lax.Precision.HIGHEST
    ).reshape(rows.shape)
    right_mats = jnp.broadcast_to(right_mat, (levels,) + right_mat.shape)
    right_out = jnp.einsum(
        "ayb,abn->ayn", right_mats, cube, precision=lax.Precision.HIGHEST
    ).reshape(rows.shape)
    summed = (left_out + right_out).astype(jnp.bfloat16).reshape(outgoing.shape)
    returned = lax.all_to_all(summed, "rc", split_axis=0, concat_axis=0, tiled=True)
    returned = returned.reshape(state_count, col_groups, pair_count, 2, group_width)
    ladder_rows = jnp.transpose(returned, (3, 0, 2, 1, 4)).reshape(density.shape)
    pair_index = lax.axis_index("rc") * pair_count + jnp.arange(pair_count, dtype=jnp.int32)
    level_index = jnp.arange(levels, dtype=jnp.int32)
    left_pick = (pair_index[:, None] // levels == level_index[None, :]).astype(jnp.float32)
    right_pick = (pair_index[:, None] % levels == level_index[None, :]).astype(jnp.float32)
    damping = 0.5 * (
        jnp.sum(left_pick * left_damping[None, :], axis=1)
        + jnp.sum(right_pick * right_damping[None, :], axis=1)
    )
    system_term = system_rows.astype(jnp.float32)
    ladder = ladder_rows.astype(jnp.float32)
    real_in = density[0].astype(jnp.float32)
    imag_in = density[1].astype(jnp.float32)
    energy_grid = energies[None, None, :]
    damp_grid = damping[None, :, None]
    new_real = system_term[1] + ladder[1] - energy_grid * imag_in - damp_grid * real_in
    new_imag = -system_term[0] - ladder[0] + energy_grid * real_in - damp_grid * imag_in
    return jnp.stack([new_real, new_imag]).astype(jnp.bfloat16)


def solution(mesh):
    placed = (P(None, "sys", "rc", None), P(), P(), P(), P(), P(), P(), P(), P(), P(), P(), P())
    return jax.shard_map(
        shards, mesh=mesh, in_specs=placed, out_specs=P(None, "sys", "rc", None), check_vma=False
    )
```

```python
import math

import jax
import jax.numpy as jnp
from jax import lax
from jax.sharding import Mesh, PartitionSpec as P


def symmetric(matrix, factor):
    widened = matrix.astype(jnp.float32)
    return ((widened + factor * widened.T) * 0.5).astype(jnp.bfloat16)


def ladder_local(regrouped, left_ops, right_ops, left_gain, right_gain, levels):
    item_count, group_count, all_pairs, column_count = regrouped.shape
    widened = regrouped.reshape(item_count, group_count, levels, levels * column_count)
    left_all = jnp.einsum("xa,ksam->ksxm", left_ops, widened, preferred_element_type=jnp.float32)
    left_term = left_all[:, :, :levels] + left_gain[None, :, None, None] * left_all[:, :, levels:]
    deepened = regrouped.reshape(item_count, group_count, levels, levels, column_count)
    right_all = jnp.einsum(
        "yb,ksabc->ksayc", right_ops, deepened, preferred_element_type=jnp.float32
    )
    right_term = (
        right_all[:, :, :, :levels]
        + right_gain[None, :, None, None, None] * right_all[:, :, :, levels:]
    )
    summed = left_term.reshape(
        item_count, group_count, all_pairs, column_count
    ) + right_term.reshape(item_count, group_count, all_pairs, column_count)
    return summed.astype(jnp.bfloat16)


def shards(
    density,
    system_real,
    system_imag,
    left_ham,
    left_coupling,
    right_ham,
    right_coupling,
    left_strength,
    right_strength,
    left_damping,
    right_damping,
    energies,
):
    herm_real = symmetric(system_real, 1.0)
    herm_imag = symmetric(system_imag, -1.0)
    levels = left_ham.shape[0]
    left_ops = jnp.concatenate([symmetric(left_ham, 1.0), symmetric(left_coupling, 1.0)], axis=0)
    right_ops = jnp.concatenate([symmetric(right_ham, 1.0), symmetric(right_coupling, 1.0)], axis=0)
    state_count = density.shape[1]
    pair_count = density.shape[2]
    column_total = density.shape[3]
    first_state = lax.axis_index(("zl", "core")) * state_count
    left_gain = lax.dynamic_slice_in_dim(left_strength, first_state, state_count)
    right_gain = lax.dynamic_slice_in_dim(right_strength, first_state, state_count)
    flat_local = jnp.transpose(density.reshape(2, state_count, -1), (1, 0, 2))
    gathered = lax.all_gather(flat_local.reshape(2 * state_count, -1), "zl", axis=0, tiled=True)
    gathered = lax.all_gather(gathered, "core", axis=0, tiled=True)
    own_real = lax.dynamic_slice_in_dim(herm_real, first_state, state_count, axis=0)
    own_imag = lax.dynamic_slice_in_dim(herm_imag, first_state, state_count, axis=0)
    real_rows = jnp.stack([own_real, -own_imag], axis=2).reshape(state_count, -1)
    imag_rows = jnp.stack([own_imag, own_real], axis=2).reshape(state_count, -1)
    mixer = jnp.concatenate([real_rows, imag_rows], axis=0)
    run_count = lax.axis_size("zl")
    core_count = lax.axis_size("core")
    mixer = mixer.reshape(2 * state_count, run_count, core_count, 2 * state_count)
    mixer = jnp.transpose(mixer, (0, 2, 1, 3)).reshape(2 * state_count, -1)
    product = jnp.dot(mixer, gathered, preferred_element_type=jnp.float32)
    product = lax.reduce_precision(product, exponent_bits=8, mantissa_bits=7)
    system_rows = product.astype(jnp.bfloat16).reshape(density.shape)
    rc_count = lax.axis_size(("x", "y", "zh"))
    col_groups = rc_count // state_count
    group_width = column_total // col_groups
    outgoing = density.reshape(2, state_count, pair_count, col_groups, group_width)
    outgoing = jnp.transpose(outgoing, (1, 3, 2, 0, 4)).reshape(
        rc_count, pair_count, 2, group_width
    )
    incoming = lax.all_to_all(outgoing, ("x", "y", "zh"), split_axis=0, concat_axis=0, tiled=True)
    rows = incoming.reshape(rc_count * pair_count, 2 * group_width).astype(jnp.float32)
    my_state = first_state + lax.axis_index(("x", "y", "zh")) // col_groups
    left_g = lax.dynamic_slice_in_dim(left_strength, my_state, 1)
    right_g = lax.dynamic_slice_in_dim(right_strength, my_state, 1)
    left_ops32 = left_ops.astype(jnp.float32)
    right_ops32 = right_ops.astype(jnp.float32)
    left_mat = left_ops32[:levels] + left_g * left_ops32[levels:]
    right_mat = right_ops32[:levels] + right_g * right_ops32[levels:]
    cube = rows.reshape(levels, levels, -1)
    left_out = jnp.einsum(
        "xa,abn->xbn", left_mat, cube, precision=lax.Precision.HIGHEST
    ).reshape(rows.shape)
    right_mats = jnp.broadcast_to(right_mat, (levels,) + right_mat.shape)
    right_out = jnp.einsum(
        "ayb,abn->ayn", right_mats, cube, precision=lax.Precision.HIGHEST
    ).reshape(rows.shape)
    summed = (left_out + right_out).astype(jnp.bfloat16).reshape(outgoing.shape)
    returned = lax.all_to_all(summed, ("x", "y", "zh"), split_axis=0, concat_axis=0, tiled=True)
    returned = returned.reshape(state_count, col_groups, pair_count, 2, group_width)
    ladder_rows = jnp.transpose(returned, (3, 0, 2, 1, 4)).reshape(density.shape)
    pair_index = lax.axis_index(("x", "y", "zh")) * pair_count + jnp.arange(pair_count, dtype=jnp.int32)
    level_index = jnp.arange(levels, dtype=jnp.int32)
    left_pick = (pair_index[:, None] // levels == level_index[None, :]).astype(jnp.float32)
    right_pick = (pair_index[:, None] % levels == level_index[None, :]).astype(jnp.float32)
    damping = 0.5 * (
        jnp.sum(left_pick * left_damping[None, :], axis=1)
        + jnp.sum(right_pick * right_damping[None, :], axis=1)
    )
    system_term = system_rows.astype(jnp.float32)
    ladder = ladder_rows.astype(jnp.float32)
    real_in = density[0].astype(jnp.float32)
    imag_in = density[1].astype(jnp.float32)
    energy_grid = energies[None, None, :]
    damp_grid = damping[None, :, None]
    new_real = system_term[1] + ladder[1] - energy_grid * imag_in - damp_grid * real_in
    new_imag = -system_term[0] - ladder[0] + energy_grid * real_in - damp_grid * imag_in
    return jnp.stack([new_real, new_imag]).astype(jnp.bfloat16)


def solution(mesh):
    devices = mesh.devices.reshape(4, 4, 4, 4, 2)
    split = Mesh(devices, ("x", "y", "zh", "zl", "core"))
    block = P(None, ("zl", "core"), ("x", "y", "zh"), None)
    placed = (block, P(), P(), P(), P(), P(), P(), P(), P(), P(), P(), P())
    return jax.shard_map(shards, mesh=split, in_specs=placed, out_specs=block, check_vma=False)
```

```python
import math

import jax
import jax.numpy as jnp
from jax import lax
from jax.sharding import PartitionSpec as P


def symmetric(matrix, factor):
    widened = matrix.astype(jnp.float32)
    return ((widened + factor * widened.T) * 0.5).astype(jnp.bfloat16)


def ladder_local(regrouped, left_ops, right_ops, left_gain, right_gain, levels):
    item_count, group_count, all_pairs, column_count = regrouped.shape
    widened = regrouped.reshape(item_count, group_count, levels, levels * column_count)
    left_all = jnp.einsum("xa,ksam->ksxm", left_ops, widened, preferred_element_type=jnp.float32)
    left_term = left_all[:, :, :levels] + left_gain[None, :, None, None] * left_all[:, :, levels:]
    deepened = regrouped.reshape(item_count, group_count, levels, levels, column_count)
    right_all = jnp.einsum(
        "yb,ksabc->ksayc", right_ops, deepened, preferred_element_type=jnp.float32
    )
    right_term = (
        right_all[:, :, :, :levels]
        + right_gain[None, :, None, None, None] * right_all[:, :, :, levels:]
    )
    summed = left_term.reshape(
        item_count, group_count, all_pairs, column_count
    ) + right_term.reshape(item_count, group_count, all_pairs, column_count)
    return summed.astype(jnp.bfloat16)


def shards(
    density,
    system_real,
    system_imag,
    left_ham,
    left_coupling,
    right_ham,
    right_coupling,
    left_strength,
    right_strength,
    left_damping,
    right_damping,
    energies,
):
    herm_real = symmetric(system_real, 1.0)
    herm_imag = symmetric(system_imag, -1.0)
    levels = left_ham.shape[0]
    left_ops = jnp.concatenate([symmetric(left_ham, 1.0), symmetric(left_coupling, 1.0)], axis=0)
    right_ops = jnp.concatenate([symmetric(right_ham, 1.0), symmetric(right_coupling, 1.0)], axis=0)
    state_count = density.shape[1]
    pair_count = density.shape[2]
    column_total = density.shape[3]
    first_state = lax.axis_index("sys") * state_count
    left_gain = lax.dynamic_slice_in_dim(left_strength, first_state, state_count)
    right_gain = lax.dynamic_slice_in_dim(right_strength, first_state, state_count)
    gathered = lax.all_gather(density, "sys", axis=0, tiled=False)
    sys_count = gathered.shape[0]
    own_real = lax.dynamic_slice_in_dim(herm_real, first_state, state_count, axis=0)
    own_imag = lax.dynamic_slice_in_dim(herm_imag, first_state, state_count, axis=0)
    real3 = own_real.reshape(state_count, sys_count, state_count)
    imag3 = own_imag.reshape(state_count, sys_count, state_count)
    mixer = jnp.stack(
        [jnp.stack([real3, -imag3], axis=2), jnp.stack([imag3, real3], axis=2)], axis=0
    ).reshape(2 * state_count, -1)
    product = jnp.einsum(
        "ok,kjc->ojc",
        mixer,
        gathered.reshape(-1, pair_count, column_total),
        preferred_element_type=jnp.float32,
    )
    product = lax.reduce_precision(product, exponent_bits=8, mantissa_bits=7)
    system_rows = product.astype(jnp.bfloat16).reshape(density.shape)
    rc_count = lax.axis_size("rc")
    col_groups = rc_count // state_count
    group_width = column_total // col_groups
    outgoing = density.reshape(2, state_count, pair_count, col_groups, group_width)
    outgoing = jnp.transpose(outgoing, (1, 3, 2, 0, 4)).reshape(
        rc_count, pair_count, 2, group_width
    )
    incoming = lax.all_to_all(outgoing, "rc", split_axis=0, concat_axis=0, tiled=True)
    rows = incoming.reshape(rc_count * pair_count, 2 * group_width).astype(jnp.float32)
    my_state = first_state + lax.axis_index("rc") // col_groups
    left_g = lax.dynamic_slice_in_dim(left_strength, my_state, 1)
    right_g = lax.dynamic_slice_in_dim(right_strength, my_state, 1)
    left_ops32 = left_ops.astype(jnp.float32)
    right_ops32 = right_ops.astype(jnp.float32)
    left_mat = left_ops32[:levels] + left_g * left_ops32[levels:]
    right_mat = right_ops32[:levels] + right_g * right_ops32[levels:]
    cube = rows.reshape(levels, levels, -1)
    left_out = jnp.einsum(
        "xa,abn->xbn", left_mat, cube, precision=lax.Precision.HIGHEST
    ).reshape(rows.shape)
    right_mats = jnp.broadcast_to(right_mat, (levels,) + right_mat.shape)
    right_out = jnp.einsum(
        "ayb,abn->ayn", right_mats, cube, precision=lax.Precision.HIGHEST
    ).reshape(rows.shape)
    summed = (left_out + right_out).astype(jnp.bfloat16).reshape(outgoing.shape)
    returned = lax.all_to_all(summed, "rc", split_axis=0, concat_axis=0, tiled=True)
    returned = returned.reshape(state_count, col_groups, pair_count, 2, group_width)
    ladder_rows = jnp.transpose(returned, (3, 0, 2, 1, 4)).reshape(density.shape)
    pair_index = lax.axis_index("rc") * pair_count + jnp.arange(pair_count, dtype=jnp.int32)
    level_index = jnp.arange(levels, dtype=jnp.int32)
    left_pick = (pair_index[:, None] // levels == level_index[None, :]).astype(jnp.float32)
    right_pick = (pair_index[:, None] % levels == level_index[None, :]).astype(jnp.float32)
    damping = 0.5 * (
        jnp.sum(left_pick * left_damping[None, :], axis=1)
        + jnp.sum(right_pick * right_damping[None, :], axis=1)
    )
    system_term = system_rows.astype(jnp.float32)
    ladder = ladder_rows.astype(jnp.float32)
    real_in = density[0].astype(jnp.float32)
    imag_in = density[1].astype(jnp.float32)
    energy_grid = energies[None, None, :]
    damp_grid = damping[None, :, None]
    new_real = system_term[1] + ladder[1] - energy_grid * imag_in - damp_grid * real_in
    new_imag = -system_term[0] - ladder[0] + energy_grid * real_in - damp_grid * imag_in
    return jnp.stack([new_real, new_imag]).astype(jnp.bfloat16)


def solution(mesh):
    placed = (P(None, "sys", "rc", None), P(), P(), P(), P(), P(), P(), P(), P(), P(), P(), P())
    return jax.shard_map(
        shards, mesh=mesh, in_specs=placed, out_specs=P(None, "sys", "rc", None), check_vma=False
    )
```

```python
import math

import jax
import jax.numpy as jnp
from jax import lax
from jax.sharding import PartitionSpec as P


def symmetric(matrix, factor):
    widened = matrix.astype(jnp.float32)
    return ((widened + factor * widened.T) * 0.5).astype(jnp.bfloat16)


def ladder_local(regrouped, left_ops, right_ops, left_gain, right_gain, levels):
    item_count, group_count, all_pairs, column_count = regrouped.shape
    widened = regrouped.reshape(item_count, group_count, levels, levels * column_count)
    left_all = jnp.einsum("xa,ksam->ksxm", left_ops, widened, preferred_element_type=jnp.float32)
    left_term = left_all[:, :, :levels] + left_gain[None, :, None, None] * left_all[:, :, levels:]
    deepened = regrouped.reshape(item_count, group_count, levels, levels, column_count)
    right_all = jnp.einsum(
        "yb,ksabc->ksayc", right_ops, deepened, preferred_element_type=jnp.float32
    )
    right_term = (
        right_all[:, :, :, :levels]
        + right_gain[None, :, None, None, None] * right_all[:, :, :, levels:]
    )
    summed = left_term.reshape(
        item_count, group_count, all_pairs, column_count
    ) + right_term.reshape(item_count, group_count, all_pairs, column_count)
    return summed.astype(jnp.bfloat16)


def shards(
    density,
    system_real,
    system_imag,
    left_ham,
    left_coupling,
    right_ham,
    right_coupling,
    left_strength,
    right_strength,
    left_damping,
    right_damping,
    energies,
):
    herm_real = symmetric(system_real, 1.0)
    herm_imag = symmetric(system_imag, -1.0)
    levels = left_ham.shape[0]
    left_ops = jnp.concatenate([symmetric(left_ham, 1.0), symmetric(left_coupling, 1.0)], axis=0)
    right_ops = jnp.concatenate([symmetric(right_ham, 1.0), symmetric(right_coupling, 1.0)], axis=0)
    state_count = density.shape[1]
    pair_count = density.shape[2]
    column_total = density.shape[3]
    first_state = lax.axis_index("sys") * state_count
    left_gain = lax.dynamic_slice_in_dim(left_strength, first_state, state_count)
    right_gain = lax.dynamic_slice_in_dim(right_strength, first_state, state_count)
    gathered = lax.all_gather(density, "sys", axis=0, tiled=False)
    sys_count = gathered.shape[0]
    own_real = lax.dynamic_slice_in_dim(herm_real, first_state, state_count, axis=0)
    own_imag = lax.dynamic_slice_in_dim(herm_imag, first_state, state_count, axis=0)
    real3 = own_real.reshape(state_count, sys_count, state_count)
    imag3 = own_imag.reshape(state_count, sys_count, state_count)
    mixer = jnp.stack(
        [jnp.stack([real3, -imag3], axis=2), jnp.stack([imag3, real3], axis=2)], axis=0
    ).reshape(2 * state_count, -1)
    product = jnp.einsum(
        "ok,kjc->ojc",
        mixer,
        gathered.reshape(-1, pair_count, column_total),
        preferred_element_type=jnp.float32,
    )
    product = lax.reduce_precision(product, exponent_bits=8, mantissa_bits=7)
    system_rows = product.astype(jnp.bfloat16).reshape(density.shape)
    rc_count = lax.axis_size("rc")
    col_groups = rc_count // state_count
    group_width = column_total // col_groups
    outgoing = density.reshape(2, state_count, pair_count, col_groups, group_width)
    outgoing = jnp.transpose(outgoing, (1, 3, 2, 0, 4)).reshape(
        rc_count, pair_count, 2, group_width
    )
    incoming = lax.all_to_all(
        outgoing.reshape(rc_count, 2, -1), "rc", split_axis=0, concat_axis=0, tiled=True
    )
    rows = incoming.reshape(rc_count * pair_count, 2 * group_width).astype(jnp.float32)
    my_state = first_state + lax.axis_index("rc") // col_groups
    left_g = lax.dynamic_slice_in_dim(left_strength, my_state, 1)
    right_g = lax.dynamic_slice_in_dim(right_strength, my_state, 1)
    left_ops32 = left_ops.astype(jnp.float32)
    right_ops32 = right_ops.astype(jnp.float32)
    left_mat = left_ops32[:levels] + left_g * left_ops32[levels:]
    right_mat = right_ops32[:levels] + right_g * right_ops32[levels:]
    cube = rows.reshape(levels, levels, -1)
    left_out = jnp.einsum(
        "xa,abn->xbn", left_mat, cube, precision=lax.Precision.HIGHEST
    ).reshape(rows.shape)
    right_mats = jnp.broadcast_to(right_mat, (levels,) + right_mat.shape)
    right_out = jnp.einsum(
        "ayb,abn->ayn", right_mats, cube, precision=lax.Precision.HIGHEST
    ).reshape(rows.shape)
    summed = (left_out + right_out).astype(jnp.bfloat16).reshape(rc_count, 2, -1)
    returned = lax.all_to_all(summed, "rc", split_axis=0, concat_axis=0, tiled=True)
    returned = returned.reshape(state_count, col_groups, pair_count, 2, group_width)
    ladder_rows = jnp.transpose(returned, (3, 0, 2, 1, 4)).reshape(density.shape)
    pair_index = lax.axis_index("rc") * pair_count + jnp.arange(pair_count, dtype=jnp.int32)
    level_index = jnp.arange(levels, dtype=jnp.int32)
    left_pick = (pair_index[:, None] // levels == level_index[None, :]).astype(jnp.float32)
    right_pick = (pair_index[:, None] % levels == level_index[None, :]).astype(jnp.float32)
    damping = 0.5 * (
        jnp.sum(left_pick * left_damping[None, :], axis=1)
        + jnp.sum(right_pick * right_damping[None, :], axis=1)
    )
    system_term = system_rows.astype(jnp.float32)
    ladder = ladder_rows.astype(jnp.float32)
    real_in = density[0].astype(jnp.float32)
    imag_in = density[1].astype(jnp.float32)
    energy_grid = energies[None, None, :]
    damp_grid = damping[None, :, None]
    new_real = system_term[1] + ladder[1] - energy_grid * imag_in - damp_grid * real_in
    new_imag = -system_term[0] - ladder[0] + energy_grid * real_in - damp_grid * imag_in
    return jnp.stack([new_real, new_imag]).astype(jnp.bfloat16)


def solution(mesh):
    placed = (P(None, "sys", "rc", None), P(), P(), P(), P(), P(), P(), P(), P(), P(), P(), P())
    return jax.shard_map(
        shards, mesh=mesh, in_specs=placed, out_specs=P(None, "sys", "rc", None), check_vma=False
    )
```

```python
import math

import jax
import jax.numpy as jnp
from jax import lax
from jax.sharding import PartitionSpec as P


def symmetric(matrix, factor):
    widened = matrix.astype(jnp.float32)
    return ((widened + factor * widened.T) * 0.5).astype(jnp.bfloat16)


def ladder_local(regrouped, left_ops, right_ops, left_gain, right_gain, levels):
    item_count, group_count, all_pairs, column_count = regrouped.shape
    widened = regrouped.reshape(item_count, group_count, levels, levels * column_count)
    left_all = jnp.einsum("xa,ksam->ksxm", left_ops, widened, preferred_element_type=jnp.float32)
    left_term = left_all[:, :, :levels] + left_gain[None, :, None, None] * left_all[:, :, levels:]
    deepened = regrouped.reshape(item_count, group_count, levels, levels, column_count)
    right_all = jnp.einsum(
        "yb,ksabc->ksayc", right_ops, deepened, preferred_element_type=jnp.float32
    )
    right_term = (
        right_all[:, :, :, :levels]
        + right_gain[None, :, None, None, None] * right_all[:, :, :, levels:]
    )
    summed = left_term.reshape(
        item_count, group_count, all_pairs, column_count
    ) + right_term.reshape(item_count, group_count, all_pairs, column_count)
    return summed.astype(jnp.bfloat16)


def shards(
    density,
    system_real,
    system_imag,
    left_ham,
    left_coupling,
    right_ham,
    right_coupling,
    left_strength,
    right_strength,
    left_damping,
    right_damping,
    energies,
):
    herm_real = symmetric(system_real, 1.0)
    herm_imag = symmetric(system_imag, -1.0)
    levels = left_ham.shape[0]
    left_ops = jnp.concatenate([symmetric(left_ham, 1.0), symmetric(left_coupling, 1.0)], axis=0)
    right_ops = jnp.concatenate([symmetric(right_ham, 1.0), symmetric(right_coupling, 1.0)], axis=0)
    state_count = density.shape[1]
    pair_count = density.shape[2]
    column_total = density.shape[3]
    first_state = lax.axis_index("sys") * state_count
    left_gain = lax.dynamic_slice_in_dim(left_strength, first_state, state_count)
    right_gain = lax.dynamic_slice_in_dim(right_strength, first_state, state_count)
    gathered = lax.all_gather(density, "sys", axis=0, tiled=False)
    sys_count = gathered.shape[0]
    own_real = lax.dynamic_slice_in_dim(herm_real, first_state, state_count, axis=0)
    own_imag = lax.dynamic_slice_in_dim(herm_imag, first_state, state_count, axis=0)
    real3 = own_real.reshape(state_count, sys_count, state_count)
    imag3 = own_imag.reshape(state_count, sys_count, state_count)
    mixer = jnp.stack(
        [jnp.stack([real3, -imag3], axis=2), jnp.stack([imag3, real3], axis=2)], axis=0
    ).reshape(2 * state_count, -1)
    product = jnp.einsum(
        "ok,kjc->ojc",
        mixer,
        gathered.reshape(-1, pair_count, column_total),
        preferred_element_type=jnp.float32,
    )
    product = lax.reduce_precision(product, exponent_bits=8, mantissa_bits=7)
    system_rows = product.astype(jnp.bfloat16).reshape(density.shape)
    rc_count = lax.axis_size("rc")
    col_groups = rc_count // (2 * state_count)
    group_width = column_total // col_groups
    outgoing = density.reshape(2, state_count, pair_count, col_groups, group_width)
    outgoing = jnp.transpose(outgoing, (1, 3, 0, 2, 4)).reshape(
        rc_count, pair_count, group_width
    )
    incoming = lax.all_to_all(outgoing, "rc", split_axis=0, concat_axis=0, tiled=True)
    rows = incoming.reshape(rc_count * pair_count, group_width).astype(jnp.float32)
    my_state = first_state + lax.axis_index("rc") // (2 * col_groups)
    left_g = lax.dynamic_slice_in_dim(left_strength, my_state, 1)
    right_g = lax.dynamic_slice_in_dim(right_strength, my_state, 1)
    left_ops32 = left_ops.astype(jnp.float32)
    right_ops32 = right_ops.astype(jnp.float32)
    left_mat = left_ops32[:levels] + left_g * left_ops32[levels:]
    right_mat = right_ops32[:levels] + right_g * right_ops32[levels:]
    cube = rows.reshape(levels, levels, -1)
    left_out = jnp.einsum(
        "xa,abn->xbn", left_mat, cube, precision=lax.Precision.HIGHEST
    ).reshape(rows.shape)
    right_mats = jnp.broadcast_to(right_mat, (levels,) + right_mat.shape)
    right_out = jnp.einsum(
        "ayb,abn->ayn", right_mats, cube, precision=lax.Precision.HIGHEST
    ).reshape(rows.shape)
    summed = (left_out + right_out).astype(jnp.bfloat16).reshape(outgoing.shape)
    returned = lax.all_to_all(summed, "rc", split_axis=0, concat_axis=0, tiled=True)
    returned = returned.reshape(state_count, col_groups, 2, pair_count, group_width)
    ladder_rows = jnp.transpose(returned, (2, 0, 3, 1, 4)).reshape(density.shape)
    pair_index = lax.axis_index("rc") * pair_count + jnp.arange(pair_count, dtype=jnp.int32)
    level_index = jnp.arange(levels, dtype=jnp.int32)
    left_pick = (pair_index[:, None] // levels == level_index[None, :]).astype(jnp.float32)
    right_pick = (pair_index[:, None] % levels == level_index[None, :]).astype(jnp.float32)
    damping = 0.5 * (
        jnp.sum(left_pick * left_damping[None, :], axis=1)
        + jnp.sum(right_pick * right_damping[None, :], axis=1)
    )
    system_term = system_rows.astype(jnp.float32)
    ladder = ladder_rows.astype(jnp.float32)
    real_in = density[0].astype(jnp.float32)
    imag_in = density[1].astype(jnp.float32)
    energy_grid = energies[None, None, :]
    damp_grid = damping[None, :, None]
    new_real = system_term[1] + ladder[1] - energy_grid * imag_in - damp_grid * real_in
    new_imag = -system_term[0] - ladder[0] + energy_grid * real_in - damp_grid * imag_in
    return jnp.stack([new_real, new_imag]).astype(jnp.bfloat16)


def solution(mesh):
    placed = (P(None, "sys", "rc", None), P(), P(), P(), P(), P(), P(), P(), P(), P(), P(), P())
    return jax.shard_map(
        shards, mesh=mesh, in_specs=placed, out_specs=P(None, "sys", "rc", None), check_vma=False
    )
```

```python
import math

import jax
import jax.numpy as jnp
from jax import lax
from jax.sharding import PartitionSpec as P


def symmetric(matrix, factor):
    widened = matrix.astype(jnp.float32)
    return ((widened + factor * widened.T) * 0.5).astype(jnp.bfloat16)


def ladder_local(regrouped, left_ops, right_ops, left_gain, right_gain, levels):
    item_count, group_count, all_pairs, column_count = regrouped.shape
    widened = regrouped.reshape(item_count, group_count, levels, levels * column_count)
    left_all = jnp.einsum("xa,ksam->ksxm", left_ops, widened, preferred_element_type=jnp.float32)
    left_term = left_all[:, :, :levels] + left_gain[None, :, None, None] * left_all[:, :, levels:]
    deepened = regrouped.reshape(item_count, group_count, levels, levels, column_count)
    right_all = jnp.einsum(
        "yb,ksabc->ksayc", right_ops, deepened, preferred_element_type=jnp.float32
    )
    right_term = (
        right_all[:, :, :, :levels]
        + right_gain[None, :, None, None, None] * right_all[:, :, :, levels:]
    )
    summed = left_term.reshape(
        item_count, group_count, all_pairs, column_count
    ) + right_term.reshape(item_count, group_count, all_pairs, column_count)
    return summed.astype(jnp.bfloat16)


def shards(
    density,
    system_real,
    system_imag,
    left_ham,
    left_coupling,
    right_ham,
    right_coupling,
    left_strength,
    right_strength,
    left_damping,
    right_damping,
    energies,
):
    herm_real = symmetric(system_real, 1.0)
    herm_imag = symmetric(system_imag, -1.0)
    levels = left_ham.shape[0]
    left_ops = jnp.concatenate([symmetric(left_ham, 1.0), symmetric(left_coupling, 1.0)], axis=0)
    right_ops = jnp.concatenate([symmetric(right_ham, 1.0), symmetric(right_coupling, 1.0)], axis=0)
    state_count = density.shape[1]
    pair_count = density.shape[2]
    column_total = density.shape[3]
    first_state = lax.axis_index("sys") * state_count
    left_gain = lax.dynamic_slice_in_dim(left_strength, first_state, state_count)
    right_gain = lax.dynamic_slice_in_dim(right_strength, first_state, state_count)
    gathered = lax.all_gather(density, "sys", axis=0, tiled=False)
    sys_count = gathered.shape[0]
    own_real = lax.dynamic_slice_in_dim(herm_real, first_state, state_count, axis=0)
    own_imag = lax.dynamic_slice_in_dim(herm_imag, first_state, state_count, axis=0)
    real3 = own_real.reshape(state_count, sys_count, state_count)
    imag3 = own_imag.reshape(state_count, sys_count, state_count)
    mixer = jnp.stack(
        [jnp.stack([real3, -imag3], axis=2), jnp.stack([imag3, real3], axis=2)], axis=0
    ).reshape(2 * state_count, -1)
    product = jnp.einsum(
        "ok,kjc->ojc",
        mixer,
        gathered.reshape(-1, pair_count, column_total),
        preferred_element_type=jnp.float32,
    )
    product = lax.reduce_precision(product, exponent_bits=8, mantissa_bits=7)
    system_rows = product.astype(jnp.bfloat16).reshape(density.shape)
    rc_count = lax.axis_size("rc")
    col_groups = rc_count // (2 * state_count)
    group_width = column_total // col_groups
    outgoing = density.reshape(2, state_count, pair_count, col_groups, group_width)
    outgoing = jnp.transpose(outgoing, (1, 3, 0, 2, 4)).reshape(
        rc_count, pair_count, group_width
    )
    incoming = lax.all_to_all(
        outgoing.reshape(rc_count, 2, -1), "rc", split_axis=0, concat_axis=0, tiled=True
    )
    rows = incoming.reshape(rc_count * pair_count, group_width).astype(jnp.float32)
    my_state = first_state + lax.axis_index("rc") // (2 * col_groups)
    left_g = lax.dynamic_slice_in_dim(left_strength, my_state, 1)
    right_g = lax.dynamic_slice_in_dim(right_strength, my_state, 1)
    left_ops32 = left_ops.astype(jnp.float32)
    right_ops32 = right_ops.astype(jnp.float32)
    left_mat = left_ops32[:levels] + left_g * left_ops32[levels:]
    right_mat = right_ops32[:levels] + right_g * right_ops32[levels:]
    cube = rows.reshape(levels, levels, -1)
    left_out = jnp.einsum(
        "xa,abn->xbn", left_mat, cube, precision=lax.Precision.HIGHEST
    ).reshape(rows.shape)
    right_mats = jnp.broadcast_to(right_mat, (levels,) + right_mat.shape)
    right_out = jnp.einsum(
        "ayb,abn->ayn", right_mats, cube, precision=lax.Precision.HIGHEST
    ).reshape(rows.shape)
    summed = (left_out + right_out).astype(jnp.bfloat16).reshape(rc_count, 2, -1)
    returned = lax.all_to_all(summed, "rc", split_axis=0, concat_axis=0, tiled=True)
    returned = returned.reshape(state_count, col_groups, 2, pair_count, group_width)
    ladder_rows = jnp.transpose(returned, (2, 0, 3, 1, 4)).reshape(density.shape)
    pair_index = lax.axis_index("rc") * pair_count + jnp.arange(pair_count, dtype=jnp.int32)
    level_index = jnp.arange(levels, dtype=jnp.int32)
    left_pick = (pair_index[:, None] // levels == level_index[None, :]).astype(jnp.float32)
    right_pick = (pair_index[:, None] % levels == level_index[None, :]).astype(jnp.float32)
    damping = 0.5 * (
        jnp.sum(left_pick * left_damping[None, :], axis=1)
        + jnp.sum(right_pick * right_damping[None, :], axis=1)
    )
    system_term = system_rows.astype(jnp.float32)
    ladder = ladder_rows.astype(jnp.float32)
    real_in = density[0].astype(jnp.float32)
    imag_in = density[1].astype(jnp.float32)
    energy_grid = energies[None, None, :]
    damp_grid = damping[None, :, None]
    new_real = system_term[1] + ladder[1] - energy_grid * imag_in - damp_grid * real_in
    new_imag = -system_term[0] - ladder[0] + energy_grid * real_in - damp_grid * imag_in
    return jnp.stack([new_real, new_imag]).astype(jnp.bfloat16)


def solution(mesh):
    placed = (P(None, "sys", "rc", None), P(), P(), P(), P(), P(), P(), P(), P(), P(), P(), P())
    return jax.shard_map(
        shards, mesh=mesh, in_specs=placed, out_specs=P(None, "sys", "rc", None), check_vma=False
    )
```

```python
import math

import jax
import jax.numpy as jnp
from jax import lax
from jax.sharding import PartitionSpec as P


def symmetric(matrix, factor):
    widened = matrix.astype(jnp.float32)
    return ((widened + factor * widened.T) * 0.5).astype(jnp.bfloat16)


def ladder_local(regrouped, left_ops, right_ops, left_gain, right_gain, levels):
    item_count, group_count, all_pairs, column_count = regrouped.shape
    widened = regrouped.reshape(item_count, group_count, levels, levels * column_count)
    left_all = jnp.einsum("xa,ksam->ksxm", left_ops, widened, preferred_element_type=jnp.float32)
    left_term = left_all[:, :, :levels] + left_gain[None, :, None, None] * left_all[:, :, levels:]
    deepened = regrouped.reshape(item_count, group_count, levels, levels, column_count)
    right_all = jnp.einsum(
        "yb,ksabc->ksayc", right_ops, deepened, preferred_element_type=jnp.float32
    )
    right_term = (
        right_all[:, :, :, :levels]
        + right_gain[None, :, None, None, None] * right_all[:, :, :, levels:]
    )
    summed = left_term.reshape(
        item_count, group_count, all_pairs, column_count
    ) + right_term.reshape(item_count, group_count, all_pairs, column_count)
    return summed.astype(jnp.bfloat16)


def shards(
    density,
    system_real,
    system_imag,
    left_ham,
    left_coupling,
    right_ham,
    right_coupling,
    left_strength,
    right_strength,
    left_damping,
    right_damping,
    energies,
):
    herm_real = symmetric(system_real, 1.0)
    herm_imag = symmetric(system_imag, -1.0)
    levels = left_ham.shape[0]
    left_ops = jnp.concatenate([symmetric(left_ham, 1.0), symmetric(left_coupling, 1.0)], axis=0)
    right_ops = jnp.concatenate([symmetric(right_ham, 1.0), symmetric(right_coupling, 1.0)], axis=0)
    state_count = density.shape[1]
    pair_count = density.shape[2]
    column_total = density.shape[3]
    first_state = lax.axis_index("sys") * state_count
    left_gain = lax.dynamic_slice_in_dim(left_strength, first_state, state_count)
    right_gain = lax.dynamic_slice_in_dim(right_strength, first_state, state_count)
    gathered = lax.all_gather(density, "sys", axis=0, tiled=False)
    sys_count = gathered.shape[0]
    own_real = lax.dynamic_slice_in_dim(herm_real, first_state, state_count, axis=0)
    own_imag = lax.dynamic_slice_in_dim(herm_imag, first_state, state_count, axis=0)
    real3 = own_real.reshape(state_count, sys_count, state_count)
    imag3 = own_imag.reshape(state_count, sys_count, state_count)
    mixer = jnp.stack(
        [jnp.stack([imag3, real3], axis=2), jnp.stack([real3, -imag3], axis=2)], axis=0
    ).reshape(2 * state_count, -1)
    product = jnp.einsum(
        "ok,kjc->ojc",
        mixer,
        gathered.reshape(-1, pair_count, column_total),
        preferred_element_type=jnp.float32,
    )
    product = lax.reduce_precision(product, exponent_bits=8, mantissa_bits=7)
    system_rows = product.astype(jnp.bfloat16).reshape(density.shape)
    rc_count = lax.axis_size("rc")
    col_groups = rc_count // (2 * state_count)
    group_width = column_total // col_groups
    outgoing = density.reshape(2, state_count, pair_count, col_groups, group_width)
    outgoing = jnp.transpose(outgoing, (1, 3, 0, 2, 4)).reshape(
        rc_count, pair_count, group_width
    )
    incoming = lax.all_to_all(
        outgoing.reshape(rc_count, 2, -1), "rc", split_axis=0, concat_axis=0, tiled=True
    )
    rows = incoming.reshape(rc_count * pair_count, group_width).astype(jnp.float32)
    my_state = first_state + lax.axis_index("rc") // (2 * col_groups)
    left_g = lax.dynamic_slice_in_dim(left_strength, my_state, 1)
    right_g = lax.dynamic_slice_in_dim(right_strength, my_state, 1)
    left_ops32 = left_ops.astype(jnp.float32)
    right_ops32 = right_ops.astype(jnp.float32)
    left_mat = left_ops32[:levels] + left_g * left_ops32[levels:]
    right_mat = right_ops32[:levels] + right_g * right_ops32[levels:]
    cube = rows.reshape(levels, levels, -1)
    left_out = jnp.einsum(
        "xa,abn->xbn", left_mat, cube, precision=lax.Precision.HIGHEST
    ).reshape(rows.shape)
    right_mats = jnp.broadcast_to(right_mat, (levels,) + right_mat.shape)
    right_out = jnp.einsum(
        "ayb,abn->ayn", right_mats, cube, precision=lax.Precision.HIGHEST
    ).reshape(rows.shape)
    summed = (left_out + right_out).astype(jnp.bfloat16).reshape(rc_count, 2, -1)
    returned = lax.all_to_all(summed, "rc", split_axis=0, concat_axis=0, tiled=True)
    returned = returned.reshape(state_count, col_groups, 2, pair_count, group_width)
    ladder_rows = jnp.transpose(returned[:, :, ::-1], (2, 0, 3, 1, 4)).reshape(density.shape)
    pair_index = lax.axis_index("rc") * pair_count + jnp.arange(pair_count, dtype=jnp.int32)
    level_index = jnp.arange(levels, dtype=jnp.int32)
    left_pick = (pair_index[:, None] // levels == level_index[None, :]).astype(jnp.float32)
    right_pick = (pair_index[:, None] % levels == level_index[None, :]).astype(jnp.float32)
    damping = 0.5 * (
        jnp.sum(left_pick * left_damping[None, :], axis=1)
        + jnp.sum(right_pick * right_damping[None, :], axis=1)
    )
    system_term = system_rows.astype(jnp.float32)
    ladder = ladder_rows.astype(jnp.float32)
    state_in = density.astype(jnp.float32)
    swapped_in = state_in[::-1]
    sign = jnp.array([1.0, -1.0], jnp.float32)[:, None, None, None]
    energy_grid = energies[None, None, None, :]
    damp_grid = damping[None, None, :, None]
    derived = sign * (system_term + ladder) - (sign * energy_grid) * swapped_in
    return (derived - damp_grid * state_in).astype(jnp.bfloat16)


def solution(mesh):
    placed = (P(None, "sys", "rc", None), P(), P(), P(), P(), P(), P(), P(), P(), P(), P(), P())
    return jax.shard_map(
        shards, mesh=mesh, in_specs=placed, out_specs=P(None, "sys", "rc", None), check_vma=False
    )
```

```python
import math

import jax
import jax.numpy as jnp
from jax import lax
from jax.sharding import PartitionSpec as P


def symmetric(matrix, factor):
    widened = matrix.astype(jnp.float32)
    return ((widened + factor * widened.T) * 0.5).astype(jnp.bfloat16)


def ladder_local(regrouped, left_ops, right_ops, left_gain, right_gain, levels):
    item_count, group_count, all_pairs, column_count = regrouped.shape
    widened = regrouped.reshape(item_count, group_count, levels, levels * column_count)
    left_all = jnp.einsum("xa,ksam->ksxm", left_ops, widened, preferred_element_type=jnp.float32)
    left_term = left_all[:, :, :levels] + left_gain[None, :, None, None] * left_all[:, :, levels:]
    deepened = regrouped.reshape(item_count, group_count, levels, levels, column_count)
    right_all = jnp.einsum(
        "yb,ksabc->ksayc", right_ops, deepened, preferred_element_type=jnp.float32
    )
    right_term = (
        right_all[:, :, :, :levels]
        + right_gain[None, :, None, None, None] * right_all[:, :, :, levels:]
    )
    summed = left_term.reshape(
        item_count, group_count, all_pairs, column_count
    ) + right_term.reshape(item_count, group_count, all_pairs, column_count)
    return summed.astype(jnp.bfloat16)


def shards(
    density,
    system_real,
    system_imag,
    left_ham,
    left_coupling,
    right_ham,
    right_coupling,
    left_strength,
    right_strength,
    left_damping,
    right_damping,
    energies,
):
    herm_real = symmetric(system_real, 1.0)
    herm_imag = symmetric(system_imag, -1.0)
    levels = left_ham.shape[0]
    left_ops = jnp.concatenate([symmetric(left_ham, 1.0), symmetric(left_coupling, 1.0)], axis=0)
    right_ops = jnp.concatenate([symmetric(right_ham, 1.0), symmetric(right_coupling, 1.0)], axis=0)
    state_count = density.shape[1]
    pair_count = density.shape[2]
    column_total = density.shape[3]
    first_state = lax.axis_index("sys") * state_count
    left_gain = lax.dynamic_slice_in_dim(left_strength, first_state, state_count)
    right_gain = lax.dynamic_slice_in_dim(right_strength, first_state, state_count)
    gathered = lax.all_gather(density, "sys", axis=0, tiled=False)
    sys_count = gathered.shape[0]
    own_real = lax.dynamic_slice_in_dim(herm_real, first_state, state_count, axis=0)
    own_imag = lax.dynamic_slice_in_dim(herm_imag, first_state, state_count, axis=0)
    real3 = own_real.reshape(state_count, sys_count, state_count)
    imag3 = own_imag.reshape(state_count, sys_count, state_count)
    mixer = jnp.stack(
        [jnp.stack([real3, -imag3], axis=2), jnp.stack([imag3, real3], axis=2)], axis=0
    ).reshape(2 * state_count, -1)
    product = jnp.einsum(
        "ok,kjc->ojc",
        mixer,
        gathered.reshape(-1, pair_count, column_total),
        preferred_element_type=jnp.float32,
    )
    product = lax.reduce_precision(product, exponent_bits=8, mantissa_bits=7)
    system_rows = product.astype(jnp.bfloat16).reshape(density.shape)
    rc_count = lax.axis_size("rc")
    col_groups = rc_count // (2 * state_count)
    group_width = column_total // col_groups
    outgoing = density.reshape(2, state_count, pair_count, col_groups, group_width)
    outgoing = jnp.transpose(outgoing, (1, 3, 0, 2, 4)).reshape(
        rc_count, pair_count, group_width
    )
    incoming = lax.all_to_all(
        outgoing.reshape(rc_count, 2, -1), "rc", split_axis=0, concat_axis=0, tiled=True
    )
    my_state = first_state + lax.axis_index("rc") // (2 * col_groups)
    left_g = lax.dynamic_slice_in_dim(left_strength, my_state, 1)
    right_g = lax.dynamic_slice_in_dim(right_strength, my_state, 1)
    left_ops32 = left_ops.astype(jnp.float32)
    right_ops32 = right_ops.astype(jnp.float32)
    left_mat = left_ops32[:levels] + left_g * left_ops32[levels:]
    right_mat = right_ops32[:levels] + right_g * right_ops32[levels:]
    cube = incoming.reshape(levels, levels, -1)

    def split_dot(spec, operator, operand):
        high = operator.astype(jnp.bfloat16)
        low = (operator - high.astype(jnp.float32)).astype(jnp.bfloat16)
        first = jnp.einsum(spec, high, operand, preferred_element_type=jnp.float32)
        return first + jnp.einsum(spec, low, operand, preferred_element_type=jnp.float32)

    left_out = split_dot("xa,abn->xbn", left_mat, cube)
    right_mats = jnp.broadcast_to(right_mat, (levels,) + right_mat.shape)
    right_out = split_dot("ayb,abn->ayn", right_mats, cube)
    summed = (left_out + right_out).astype(jnp.bfloat16).reshape(rc_count, 2, -1)
    returned = lax.all_to_all(summed, "rc", split_axis=0, concat_axis=0, tiled=True)
    returned = returned.reshape(state_count, col_groups, 2, pair_count, group_width)
    ladder_rows = jnp.transpose(returned, (2, 0, 3, 1, 4)).reshape(density.shape)
    pair_index = lax.axis_index("rc") * pair_count + jnp.arange(pair_count, dtype=jnp.int32)
    level_index = jnp.arange(levels, dtype=jnp.int32)
    left_pick = (pair_index[:, None] // levels == level_index[None, :]).astype(jnp.float32)
    right_pick = (pair_index[:, None] % levels == level_index[None, :]).astype(jnp.float32)
    damping = 0.5 * (
        jnp.sum(left_pick * left_damping[None, :], axis=1)
        + jnp.sum(right_pick * right_damping[None, :], axis=1)
    )
    system_term = system_rows.astype(jnp.float32)
    ladder = ladder_rows.astype(jnp.float32)
    real_in = density[0].astype(jnp.float32)
    imag_in = density[1].astype(jnp.float32)
    energy_grid = energies[None, None, :]
    damp_grid = damping[None, :, None]
    new_real = system_term[1] + ladder[1] - energy_grid * imag_in - damp_grid * real_in
    new_imag = -system_term[0] - ladder[0] + energy_grid * real_in - damp_grid * imag_in
    return jnp.stack([new_real, new_imag]).astype(jnp.bfloat16)


def solution(mesh):
    placed = (P(None, "sys", "rc", None), P(), P(), P(), P(), P(), P(), P(), P(), P(), P(), P())
    return jax.shard_map(
        shards, mesh=mesh, in_specs=placed, out_specs=P(None, "sys", "rc", None), check_vma=False
    )
```

```python
import math

import jax
import jax.numpy as jnp
from jax import lax
from jax.sharding import PartitionSpec as P


def symmetric(matrix, factor):
    widened = matrix.astype(jnp.float32)
    return ((widened + factor * widened.T) * 0.5).astype(jnp.bfloat16)


def ladder_local(regrouped, left_ops, right_ops, left_gain, right_gain, levels):
    item_count, group_count, all_pairs, column_count = regrouped.shape
    widened = regrouped.reshape(item_count, group_count, levels, levels * column_count)
    left_all = jnp.einsum("xa,ksam->ksxm", left_ops, widened, preferred_element_type=jnp.float32)
    left_term = left_all[:, :, :levels] + left_gain[None, :, None, None] * left_all[:, :, levels:]
    deepened = regrouped.reshape(item_count, group_count, levels, levels, column_count)
    right_all = jnp.einsum(
        "yb,ksabc->ksayc", right_ops, deepened, preferred_element_type=jnp.float32
    )
    right_term = (
        right_all[:, :, :, :levels]
        + right_gain[None, :, None, None, None] * right_all[:, :, :, levels:]
    )
    summed = left_term.reshape(
        item_count, group_count, all_pairs, column_count
    ) + right_term.reshape(item_count, group_count, all_pairs, column_count)
    return summed.astype(jnp.bfloat16)


def shards(
    density,
    system_real,
    system_imag,
    left_ham,
    left_coupling,
    right_ham,
    right_coupling,
    left_strength,
    right_strength,
    left_damping,
    right_damping,
    energies,
):
    herm_real = symmetric(system_real, 1.0)
    herm_imag = symmetric(system_imag, -1.0)
    levels = left_ham.shape[0]
    left_ops = jnp.concatenate([symmetric(left_ham, 1.0), symmetric(left_coupling, 1.0)], axis=0)
    right_ops = jnp.concatenate([symmetric(right_ham, 1.0), symmetric(right_coupling, 1.0)], axis=0)
    state_count = density.shape[1]
    pair_count = density.shape[2]
    column_total = density.shape[3]
    first_state = lax.axis_index("sys") * state_count
    left_gain = lax.dynamic_slice_in_dim(left_strength, first_state, state_count)
    right_gain = lax.dynamic_slice_in_dim(right_strength, first_state, state_count)
    gathered = lax.all_gather(density, "sys", axis=0, tiled=False)
    sys_count = gathered.shape[0]
    own_real = lax.dynamic_slice_in_dim(herm_real, first_state, state_count, axis=0)
    own_imag = lax.dynamic_slice_in_dim(herm_imag, first_state, state_count, axis=0)
    real3 = own_real.reshape(state_count, sys_count, state_count)
    imag3 = own_imag.reshape(state_count, sys_count, state_count)
    flat_gathered = gathered.reshape(-1, pair_count, column_total)
    mixers = (
        jnp.stack([real3, -imag3], axis=2).reshape(state_count, -1),
        jnp.stack([imag3, real3], axis=2).reshape(state_count, -1),
    )
    parts = []
    for mixer in mixers:
        part = jnp.einsum(
            "ok,kjc->ojc", mixer, flat_gathered, preferred_element_type=jnp.float32
        )
        part = lax.reduce_precision(part, exponent_bits=8, mantissa_bits=7)
        parts.append(part.astype(jnp.bfloat16))
    rc_count = lax.axis_size("rc")
    col_groups = rc_count // (2 * state_count)
    group_width = column_total // col_groups
    outgoing = density.reshape(2, state_count, pair_count, col_groups, group_width)
    outgoing = jnp.transpose(outgoing, (1, 3, 0, 2, 4)).reshape(
        rc_count, pair_count, group_width
    )
    incoming = lax.all_to_all(
        outgoing.reshape(rc_count, 2, -1), "rc", split_axis=0, concat_axis=0, tiled=True
    )
    rows = incoming.reshape(rc_count * pair_count, group_width).astype(jnp.float32)
    my_state = first_state + lax.axis_index("rc") // (2 * col_groups)
    left_g = lax.dynamic_slice_in_dim(left_strength, my_state, 1)
    right_g = lax.dynamic_slice_in_dim(right_strength, my_state, 1)
    left_ops32 = left_ops.astype(jnp.float32)
    right_ops32 = right_ops.astype(jnp.float32)
    left_mat = left_ops32[:levels] + left_g * left_ops32[levels:]
    right_mat = right_ops32[:levels] + right_g * right_ops32[levels:]
    cube = rows.reshape(levels, levels, -1)
    left_out = jnp.einsum(
        "xa,abn->xbn", left_mat, cube, precision=lax.Precision.HIGHEST
    ).reshape(rows.shape)
    right_mats = jnp.broadcast_to(right_mat, (levels,) + right_mat.shape)
    right_out = jnp.einsum(
        "ayb,abn->ayn", right_mats, cube, precision=lax.Precision.HIGHEST
    ).reshape(rows.shape)
    summed = (left_out + right_out).astype(jnp.bfloat16).reshape(rc_count, 2, -1)
    returned = lax.all_to_all(summed, "rc", split_axis=0, concat_axis=0, tiled=True)
    returned = returned.reshape(state_count, col_groups, 2, pair_count, group_width)
    ladder_rows = jnp.transpose(returned, (2, 0, 3, 1, 4)).reshape(density.shape)
    pair_index = lax.axis_index("rc") * pair_count + jnp.arange(pair_count, dtype=jnp.int32)
    level_index = jnp.arange(levels, dtype=jnp.int32)
    left_pick = (pair_index[:, None] // levels == level_index[None, :]).astype(jnp.float32)
    right_pick = (pair_index[:, None] % levels == level_index[None, :]).astype(jnp.float32)
    damping = 0.5 * (
        jnp.sum(left_pick * left_damping[None, :], axis=1)
        + jnp.sum(right_pick * right_damping[None, :], axis=1)
    )
    ladder = ladder_rows.astype(jnp.float32)
    real_in = density[0].astype(jnp.float32)
    imag_in = density[1].astype(jnp.float32)
    energy_grid = energies[None, None, :]
    damp_grid = damping[None, :, None]
    new_real = parts[1].astype(jnp.float32) + ladder[1] - energy_grid * imag_in - damp_grid * real_in
    new_imag = -parts[0].astype(jnp.float32) - ladder[0] + energy_grid * real_in - damp_grid * imag_in
    return jnp.stack([new_real, new_imag]).astype(jnp.bfloat16)


def solution(mesh):
    placed = (P(None, "sys", "rc", None), P(), P(), P(), P(), P(), P(), P(), P(), P(), P(), P())
    return jax.shard_map(
        shards, mesh=mesh, in_specs=placed, out_specs=P(None, "sys", "rc", None), check_vma=False
    )
```

```python
import math

import jax
import jax.numpy as jnp
from jax import lax
from jax.sharding import PartitionSpec as P


def symmetric(matrix, factor):
    widened = matrix.astype(jnp.float32)
    return ((widened + factor * widened.T) * 0.5).astype(jnp.bfloat16)


def ladder_local(regrouped, left_ops, right_ops, left_gain, right_gain, levels):
    item_count, group_count, all_pairs, column_count = regrouped.shape
    widened = regrouped.reshape(item_count, group_count, levels, levels * column_count)
    left_all = jnp.einsum("xa,ksam->ksxm", left_ops, widened, preferred_element_type=jnp.float32)
    left_term = left_all[:, :, :levels] + left_gain[None, :, None, None] * left_all[:, :, levels:]
    deepened = regrouped.reshape(item_count, group_count, levels, levels, column_count)
    right_all = jnp.einsum(
        "yb,ksabc->ksayc", right_ops, deepened, preferred_element_type=jnp.float32
    )
    right_term = (
        right_all[:, :, :, :levels]
        + right_gain[None, :, None, None, None] * right_all[:, :, :, levels:]
    )
    summed = left_term.reshape(
        item_count, group_count, all_pairs, column_count
    ) + right_term.reshape(item_count, group_count, all_pairs, column_count)
    return summed.astype(jnp.bfloat16)


def shards(
    density,
    system_real,
    system_imag,
    left_ham,
    left_coupling,
    right_ham,
    right_coupling,
    left_strength,
    right_strength,
    left_damping,
    right_damping,
    energies,
):
    herm_real = symmetric(system_real, 1.0)
    herm_imag = symmetric(system_imag, -1.0)
    levels = left_ham.shape[0]
    left_ops = jnp.concatenate([symmetric(left_ham, 1.0), symmetric(left_coupling, 1.0)], axis=0)
    right_ops = jnp.concatenate([symmetric(right_ham, 1.0), symmetric(right_coupling, 1.0)], axis=0)
    state_count = density.shape[1]
    pair_count = density.shape[2]
    column_total = density.shape[3]
    first_state = lax.axis_index("sys") * state_count
    left_gain = lax.dynamic_slice_in_dim(left_strength, first_state, state_count)
    right_gain = lax.dynamic_slice_in_dim(right_strength, first_state, state_count)
    gathered = lax.all_gather(density, "sys", axis=0, tiled=False)
    sys_count = gathered.shape[0]
    own_real = lax.dynamic_slice_in_dim(herm_real, first_state, state_count, axis=0)
    own_imag = lax.dynamic_slice_in_dim(herm_imag, first_state, state_count, axis=0)
    real3 = own_real.reshape(state_count, sys_count, state_count)
    imag3 = own_imag.reshape(state_count, sys_count, state_count)
    mixer = jnp.stack(
        [jnp.stack([real3, -imag3], axis=2), jnp.stack([imag3, real3], axis=2)], axis=0
    ).reshape(2 * state_count, -1)
    product = jnp.einsum(
        "ok,kjc->ojc",
        mixer,
        gathered.reshape(-1, pair_count, column_total),
        preferred_element_type=jnp.float32,
    )
    product = lax.reduce_precision(product, exponent_bits=8, mantissa_bits=7)
    system_rows = product.astype(jnp.bfloat16).reshape(density.shape)
    rc_count = lax.axis_size("rc")
    col_groups = rc_count // (2 * state_count)
    group_width = column_total // col_groups
    outgoing = density.reshape(2, state_count, pair_count, col_groups, group_width)
    outgoing = jnp.transpose(outgoing, (1, 3, 0, 2, 4)).reshape(
        rc_count, pair_count, group_width
    )
    incoming = lax.all_to_all(
        outgoing.reshape(rc_count, 2, -1), "rc", split_axis=0, concat_axis=0, tiled=True
    )
    rows = incoming.reshape(rc_count * pair_count, group_width).astype(jnp.float32)
    my_state = first_state + lax.axis_index("rc") // (2 * col_groups)
    left_g = lax.dynamic_slice_in_dim(left_strength, my_state, 1)
    right_g = lax.dynamic_slice_in_dim(right_strength, my_state, 1)
    left_ops32 = left_ops.astype(jnp.float32)
    right_ops32 = right_ops.astype(jnp.float32)
    left_mat = left_ops32[:levels] + left_g * left_ops32[levels:]
    right_mat = right_ops32[:levels] + right_g * right_ops32[levels:]
    cube = rows.reshape(levels, levels, -1)
    left_out = jnp.einsum(
        "xa,abn->xbn", left_mat, cube, precision=lax.Precision.HIGH
    ).reshape(rows.shape)
    right_mats = jnp.broadcast_to(right_mat, (levels,) + right_mat.shape)
    right_out = jnp.einsum(
        "ayb,abn->ayn", right_mats, cube, precision=lax.Precision.HIGH
    ).reshape(rows.shape)
    summed = (left_out + right_out).astype(jnp.bfloat16).reshape(rc_count, 2, -1)
    returned = lax.all_to_all(summed, "rc", split_axis=0, concat_axis=0, tiled=True)
    returned = returned.reshape(state_count, col_groups, 2, pair_count, group_width)
    ladder_rows = jnp.transpose(returned, (2, 0, 3, 1, 4)).reshape(density.shape)
    pair_index = lax.axis_index("rc") * pair_count + jnp.arange(pair_count, dtype=jnp.int32)
    level_index = jnp.arange(levels, dtype=jnp.int32)
    left_pick = (pair_index[:, None] // levels == level_index[None, :]).astype(jnp.float32)
    right_pick = (pair_index[:, None] % levels == level_index[None, :]).astype(jnp.float32)
    damping = 0.5 * (
        jnp.sum(left_pick * left_damping[None, :], axis=1)
        + jnp.sum(right_pick * right_damping[None, :], axis=1)
    )
    system_term = system_rows.astype(jnp.float32)
    ladder = ladder_rows.astype(jnp.float32)
    real_in = density[0].astype(jnp.float32)
    imag_in = density[1].astype(jnp.float32)
    energy_grid = energies[None, None, :]
    damp_grid = damping[None, :, None]
    new_real = system_term[1] + ladder[1] - energy_grid * imag_in - damp_grid * real_in
    new_imag = -system_term[0] - ladder[0] + energy_grid * real_in - damp_grid * imag_in
    return jnp.stack([new_real, new_imag]).astype(jnp.bfloat16)


def solution(mesh):
    placed = (P(None, "sys", "rc", None), P(), P(), P(), P(), P(), P(), P(), P(), P(), P(), P())
    return jax.shard_map(
        shards, mesh=mesh, in_specs=placed, out_specs=P(None, "sys", "rc", None), check_vma=False
    )
```

```python
import math

import jax
import jax.numpy as jnp
from jax import lax
from jax.sharding import PartitionSpec as P


def symmetric(matrix, factor):
    widened = matrix.astype(jnp.float32)
    return ((widened + factor * widened.T) * 0.5).astype(jnp.bfloat16)


def ladder_local(regrouped, left_ops, right_ops, left_gain, right_gain, levels):
    item_count, group_count, all_pairs, column_count = regrouped.shape
    widened = regrouped.reshape(item_count, group_count, levels, levels * column_count)
    left_all = jnp.einsum("xa,ksam->ksxm", left_ops, widened, preferred_element_type=jnp.float32)
    left_term = left_all[:, :, :levels] + left_gain[None, :, None, None] * left_all[:, :, levels:]
    deepened = regrouped.reshape(item_count, group_count, levels, levels, column_count)
    right_all = jnp.einsum(
        "yb,ksabc->ksayc", right_ops, deepened, preferred_element_type=jnp.float32
    )
    right_term = (
        right_all[:, :, :, :levels]
        + right_gain[None, :, None, None, None] * right_all[:, :, :, levels:]
    )
    summed = left_term.reshape(
        item_count, group_count, all_pairs, column_count
    ) + right_term.reshape(item_count, group_count, all_pairs, column_count)
    return summed.astype(jnp.bfloat16)


def shards(
    density,
    system_real,
    system_imag,
    left_ham,
    left_coupling,
    right_ham,
    right_coupling,
    left_strength,
    right_strength,
    left_damping,
    right_damping,
    energies,
):
    herm_real = symmetric(system_real, 1.0)
    herm_imag = symmetric(system_imag, -1.0)
    levels = left_ham.shape[0]
    left_ops = jnp.concatenate([symmetric(left_ham, 1.0), symmetric(left_coupling, 1.0)], axis=0)
    right_ops = jnp.concatenate([symmetric(right_ham, 1.0), symmetric(right_coupling, 1.0)], axis=0)
    state_count = density.shape[1]
    pair_count = density.shape[2]
    column_total = density.shape[3]
    first_state = lax.axis_index("sys") * state_count
    left_gain = lax.dynamic_slice_in_dim(left_strength, first_state, state_count)
    right_gain = lax.dynamic_slice_in_dim(right_strength, first_state, state_count)
    gathered = lax.all_gather(density, "sys", axis=0, tiled=False)
    sys_count = gathered.shape[0]
    own_real = lax.dynamic_slice_in_dim(herm_real, first_state, state_count, axis=0)
    own_imag = lax.dynamic_slice_in_dim(herm_imag, first_state, state_count, axis=0)
    real3 = own_real.reshape(state_count, sys_count, state_count)
    imag3 = own_imag.reshape(state_count, sys_count, state_count)
    mixer = jnp.stack(
        [jnp.stack([real3, -imag3], axis=2), jnp.stack([imag3, real3], axis=2)], axis=0
    ).reshape(2 * state_count, -1)
    product = jnp.einsum(
        "ok,kjc->ojc",
        mixer,
        gathered.reshape(-1, pair_count, column_total),
        preferred_element_type=jnp.float32,
    )
    product = lax.reduce_precision(product, exponent_bits=8, mantissa_bits=7)
    system_rows = product.astype(jnp.bfloat16).reshape(density.shape)
    rc_count = lax.axis_size("rc")
    col_groups = rc_count // (2 * state_count)
    group_width = column_total // col_groups
    outgoing = density.reshape(2, state_count, pair_count, col_groups, group_width)
    outgoing = jnp.transpose(outgoing, (1, 3, 0, 2, 4)).reshape(
        rc_count, pair_count, group_width
    )
    incoming = lax.all_to_all(
        outgoing.reshape(rc_count, 2, -1), "rc", split_axis=0, concat_axis=0, tiled=True
    )
    rows = incoming.reshape(rc_count * pair_count, group_width).astype(jnp.float32)
    my_state = first_state + lax.axis_index("rc") // (2 * col_groups)
    left_g = lax.dynamic_slice_in_dim(left_strength, my_state, 1)
    right_g = lax.dynamic_slice_in_dim(right_strength, my_state, 1)
    left_ops32 = left_ops.astype(jnp.float32)
    right_ops32 = right_ops.astype(jnp.float32)
    left_mat = left_ops32[:levels] + left_g * left_ops32[levels:]
    right_mat = right_ops32[:levels] + right_g * right_ops32[levels:]
    cube = rows.reshape(levels, levels, -1)
    right_mats = jnp.broadcast_to(right_mat, (levels,) + right_mat.shape)
    left_out = jnp.einsum(
        "xa,abn->xbn", left_mat, cube, precision=lax.Precision.HIGHEST
    ).reshape(rows.shape)
    right_out = jnp.einsum(
        "ayb,abn->ayn", right_mats, cube, precision=lax.Precision.HIGHEST
    ).reshape(rows.shape)
    summed = (right_out + left_out).astype(jnp.bfloat16).reshape(rc_count, 2, -1)
    returned = lax.all_to_all(summed, "rc", split_axis=0, concat_axis=0, tiled=True)
    returned = returned.reshape(state_count, col_groups, 2, pair_count, group_width)
    ladder_rows = jnp.transpose(returned, (2, 0, 3, 1, 4)).reshape(density.shape)
    pair_index = lax.axis_index("rc") * pair_count + jnp.arange(pair_count, dtype=jnp.int32)
    level_index = jnp.arange(levels, dtype=jnp.int32)
    left_pick = (pair_index[:, None] // levels == level_index[None, :]).astype(jnp.float32)
    right_pick = (pair_index[:, None] % levels == level_index[None, :]).astype(jnp.float32)
    damping = 0.5 * (
        jnp.sum(left_pick * left_damping[None, :], axis=1)
        + jnp.sum(right_pick * right_damping[None, :], axis=1)
    )
    system_term = system_rows.astype(jnp.float32)
    ladder = ladder_rows.astype(jnp.float32)
    real_in = density[0].astype(jnp.float32)
    imag_in = density[1].astype(jnp.float32)
    energy_grid = energies[None, None, :]
    damp_grid = damping[None, :, None]
    new_real = system_term[1] + ladder[1] - energy_grid * imag_in - damp_grid * real_in
    new_imag = -system_term[0] - ladder[0] + energy_grid * real_in - damp_grid * imag_in
    return jnp.stack([new_real, new_imag]).astype(jnp.bfloat16)


def solution(mesh):
    placed = (P(None, "sys", "rc", None), P(), P(), P(), P(), P(), P(), P(), P(), P(), P(), P())
    return jax.shard_map(
        shards, mesh=mesh, in_specs=placed, out_specs=P(None, "sys", "rc", None), check_vma=False
    )
```

```python
import math

import jax
import jax.numpy as jnp
from jax import lax
from jax.sharding import PartitionSpec as P


def symmetric(matrix, factor):
    widened = matrix.astype(jnp.float32)
    return ((widened + factor * widened.T) * 0.5).astype(jnp.bfloat16)


def ladder_local(regrouped, left_ops, right_ops, left_gain, right_gain, levels):
    item_count, group_count, all_pairs, column_count = regrouped.shape
    widened = regrouped.reshape(item_count, group_count, levels, levels * column_count)
    left_all = jnp.einsum("xa,ksam->ksxm", left_ops, widened, preferred_element_type=jnp.float32)
    left_term = left_all[:, :, :levels] + left_gain[None, :, None, None] * left_all[:, :, levels:]
    deepened = regrouped.reshape(item_count, group_count, levels, levels, column_count)
    right_all = jnp.einsum(
        "yb,ksabc->ksayc", right_ops, deepened, preferred_element_type=jnp.float32
    )
    right_term = (
        right_all[:, :, :, :levels]
        + right_gain[None, :, None, None, None] * right_all[:, :, :, levels:]
    )
    summed = left_term.reshape(
        item_count, group_count, all_pairs, column_count
    ) + right_term.reshape(item_count, group_count, all_pairs, column_count)
    return summed.astype(jnp.bfloat16)


def shards(
    density,
    system_real,
    system_imag,
    left_ham,
    left_coupling,
    right_ham,
    right_coupling,
    left_strength,
    right_strength,
    left_damping,
    right_damping,
    energies,
):
    herm_real = symmetric(system_real, 1.0)
    herm_imag = symmetric(system_imag, -1.0)
    levels = left_ham.shape[0]
    left_ops = jnp.concatenate([symmetric(left_ham, 1.0), symmetric(left_coupling, 1.0)], axis=0)
    right_ops = jnp.concatenate([symmetric(right_ham, 1.0), symmetric(right_coupling, 1.0)], axis=0)
    state_count = density.shape[1]
    pair_count = density.shape[2]
    column_total = density.shape[3]
    first_state = lax.axis_index("sys") * state_count
    left_gain = lax.dynamic_slice_in_dim(left_strength, first_state, state_count)
    right_gain = lax.dynamic_slice_in_dim(right_strength, first_state, state_count)
    gathered = lax.all_gather(density, "sys", axis=0, tiled=False)
    sys_count = gathered.shape[0]
    own_real = lax.dynamic_slice_in_dim(herm_real, first_state, state_count, axis=0)
    own_imag = lax.dynamic_slice_in_dim(herm_imag, first_state, state_count, axis=0)
    real3 = own_real.reshape(state_count, sys_count, state_count)
    imag3 = own_imag.reshape(state_count, sys_count, state_count)
    mixer = jnp.stack(
        [jnp.stack([imag3, real3], axis=2), jnp.stack([real3, -imag3], axis=2)], axis=0
    ).reshape(2 * state_count, -1)
    product = jnp.einsum(
        "ok,kjc->ojc",
        mixer,
        gathered.reshape(-1, pair_count, column_total),
        preferred_element_type=jnp.float32,
    )
    product = lax.reduce_precision(product, exponent_bits=8, mantissa_bits=7)
    system_rows = product.astype(jnp.bfloat16).reshape(density.shape)
    rc_count = lax.axis_size("rc")
    col_groups = rc_count // (2 * state_count)
    group_width = column_total // col_groups
    outgoing = density.reshape(2, state_count, pair_count, col_groups, group_width)
    outgoing = jnp.transpose(outgoing, (1, 3, 0, 2, 4)).reshape(
        rc_count, pair_count, group_width
    )
    incoming = lax.all_to_all(
        outgoing.reshape(rc_count, 2, -1), "rc", split_axis=0, concat_axis=0, tiled=True
    )
    rows = incoming.reshape(rc_count * pair_count, group_width).astype(jnp.float32)
    my_state = first_state + lax.axis_index("rc") // (2 * col_groups)
    left_g = lax.dynamic_slice_in_dim(left_strength, my_state, 1)
    right_g = lax.dynamic_slice_in_dim(right_strength, my_state, 1)
    left_ops32 = left_ops.astype(jnp.float32)
    right_ops32 = right_ops.astype(jnp.float32)
    left_mat = left_ops32[:levels] + left_g * left_ops32[levels:]
    right_mat = right_ops32[:levels] + right_g * right_ops32[levels:]
    cube = rows.reshape(levels, levels, -1)
    right_mats = jnp.broadcast_to(right_mat, (levels,) + right_mat.shape)
    left_out = jnp.einsum(
        "xa,abn->xbn", left_mat, cube, precision=lax.Precision.HIGHEST
    ).reshape(rows.shape)
    right_out = jnp.einsum(
        "ayb,abn->ayn", right_mats, cube, precision=lax.Precision.HIGHEST
    ).reshape(rows.shape)
    summed = (right_out + left_out).astype(jnp.bfloat16).reshape(rc_count, 2, -1)
    returned = lax.all_to_all(summed, "rc", split_axis=0, concat_axis=0, tiled=True)
    returned = returned.reshape(state_count, col_groups, 2, pair_count, group_width)
    ladder_rows = jnp.transpose(returned[:, :, ::-1], (2, 0, 3, 1, 4)).reshape(density.shape)
    pair_index = lax.axis_index("rc") * pair_count + jnp.arange(pair_count, dtype=jnp.int32)
    level_index = jnp.arange(levels, dtype=jnp.int32)
    left_pick = (pair_index[:, None] // levels == level_index[None, :]).astype(jnp.float32)
    right_pick = (pair_index[:, None] % levels == level_index[None, :]).astype(jnp.float32)
    damping = 0.5 * (
        jnp.sum(left_pick * left_damping[None, :], axis=1)
        + jnp.sum(right_pick * right_damping[None, :], axis=1)
    )
    system_term = system_rows.astype(jnp.float32)
    ladder = ladder_rows.astype(jnp.float32)
    state_in = density.astype(jnp.float32)
    swapped_in = state_in[::-1]
    sign = jnp.array([1.0, -1.0], jnp.float32)[:, None, None, None]
    energy_grid = energies[None, None, None, :]
    damp_grid = damping[None, None, :, None]
    derived = sign * (system_term + ladder) - (sign * energy_grid) * swapped_in
    return (derived - damp_grid * state_in).astype(jnp.bfloat16)


def solution(mesh):
    placed = (P(None, "sys", "rc", None), P(), P(), P(), P(), P(), P(), P(), P(), P(), P(), P())
    return jax.shard_map(
        shards, mesh=mesh, in_specs=placed, out_specs=P(None, "sys", "rc", None), check_vma=False
    )
```
